256 devices in a mesh: grp: 4 (over y), mdl: 64 (over z, x, core).
Axes of the slice: x: 4, y: 4, z: 8, core: 2. Of those that a mesh axis runs over, the one named last changes fastest.
Arguments:
- pol_hidden: bfloat16 [1024, 4096], P(('grp', 'mdl')), may hold values from -6 to 6
- ref_hidden: bfloat16 [1024, 4096], P(('grp', 'mdl')), may hold values from -6 to 6
- pol_mlp_gain: bfloat16 [4096], replicated, may hold values from 0.099609375 to 1.8984375
- ref_mlp_gain: bfloat16 [4096], replicated, may hold values from 0.099609375 to 1.8984375
- pol_final_gain: bfloat16 [4096], replicated, may hold values from 0.099609375 to 1.8984375
- ref_final_gain: bfloat16 [4096], replicated, may hold values from 0.099609375 to 1.8984375
- pol_gate: bfloat16 [4096, 11008], P(None, 'mdl'), may hold values from -0.09375 to 0.09375
- pol_up: bfloat16 [4096, 11008], P(None, 'mdl'), may hold values from -0.09375 to 0.09375
- pol_down: bfloat16 [11008, 4096], P('mdl'), may hold values from -0.109375 to 0.109375
- ref_gate: bfloat16 [4096, 11008], P(None, 'mdl'), may hold values from -0.09375 to 0.09375
- ref_up: bfloat16 [4096, 11008], P(None, 'mdl'), may hold values from -0.09375 to 0.09375
- ref_down: bfloat16 [11008, 4096], P('mdl'), may hold values from -0.109375 to 0.109375
- pol_head: bfloat16 [64000, 4096], P(('grp', 'mdl')), may hold values from -20 to 20
- ref_head: bfloat16 [64000, 4096], P(('grp', 'mdl')), may hold values from -20 to 20
- token_ids: int32 [1024], replicated, may hold values from 0 to 63999
- lengths: int32 [16], replicated, may hold values from 1 to 160, 1024 in all
Outputs:
- pol_out: bfloat16 [1024, 4096], P(('grp', 'mdl'))
- ref_out: bfloat16 [1024, 4096], P(('grp', 'mdl'))
- rollout_ratio: float32 [16], replicated
The draws below stay inside these ranges and needn't reach their ends.
Inputs may be any that keep to these rules, and one draw needn't show every extreme that they name: Rollout lengths sum to 1024; the longest is exactly 160.
All inputs are finite; a program needn't handle non-finite values.
Results may differ from the reference program's by a relative error of at most 0.012.
The reference program's roundings to bfloat16 on the way count: a program that leaves them out, or rounds other values in their place, can miss the bound.
Values may be sent and summed in bfloat16 or wider, within the bound.
No kernel may reach another device: no remote copies, remote signals or barrier semaphores. Data moves between devices by JAX's collectives and lax.ppermute only.
A program may use at most 128 MiB of HBM per device.

```python
import math
import jax
import jax.numpy as jnp
import numpy as np
from jax import lax

D = 4096
FF = 11008
V = 64000
R = 16
TOKENS = 1024
LEN_MAX = 160
N_GRP = 4


def head_rows(key):
    first = jax.random.fold_in(key, 0)
    base = jnp.clip(jax.random.normal(first, (V, D), jnp.float32), -6.0, 6.0) * (3.0 / math.sqrt(D))
    return jnp.clip(base, -20.0, 20.0)


def draw_pol_head(key, part):
    return head_rows(jax.random.fold_in(key, 11)).astype(jnp.bfloat16)


def draw_ref_head(key, part):
    return head_rows(jax.random.fold_in(key, 23)).astype(jnp.bfloat16)


def with_ends(drawn, key, least, largest):
    shape = drawn.shape
    place = [jax.random.randint(jax.random.fold_in(key, axis), (), 0, shape[axis]) for axis in range(len(shape))]
    drawn = drawn.at[tuple(place)].set(least)
    longest = shape.index(max(shape))
    place[longest] = (place[longest] + 1) % shape[longest]
    return drawn.at[tuple(place)].set(largest)


def block_scale(stream_key, shape, cuts, least, high):
    factor_of, own = 1.0, jax.random.fold_in(stream_key, 6)
    for axis_at, blocks in cuts:
        draws = jnp.exp(jax.random.uniform(jax.random.fold_in(own, axis_at), (blocks,), jnp.float32, least / len(cuts), high / len(cuts)))
        factor_of = factor_of * jnp.repeat(draws, shape[axis_at] // blocks).reshape([-1 if axis == axis_at else 1 for axis in range(len(shape))])
    return factor_of


def split_up(amount, total, limit, slope):
    portions = [(1 << 20) // math.isqrt(rank ** slope) + 1 for rank in range(2, amount + 1)]
    rest, holding = total - limit - (amount - 1), [1] * (amount - 1)
    while rest > 0:
        free = [i for i in range(amount - 1) if holding[i] < limit]
        pool, budget = sum([portions[i] for i in free]), rest
        for i in free:
            addition = min(limit - holding[i], max(1, budget * portions[i] // pool), rest)
            holding[i] = holding[i] + addition
            rest = rest - addition
    return np.array([limit] + holding)


def uneven_parts(stream_key, number_of, total, limit, skew):
    if number_of == 2:
        one = jax.random.randint(stream_key, (), max(1, total - limit), min(limit, total - 1) + 1)
        return jnp.stack([one, total - one])
    sizes = jnp.asarray(split_up(number_of, total, limit, skew), jnp.int32)
    twos = (number_of - 1) // 2
    donor, sink = sizes[1:1 + 2 * twos:2], sizes[2:2 + 2 * twos:2]
    slack = jnp.minimum(donor - 1, limit - sink)
    passed = jax.random.randint(jax.random.fold_in(stream_key, 1), (twos,), 0, 1 << 20) % (slack + 1)
    sizes = sizes.at[1:1 + 2 * twos:2].set(donor - passed).at[2:2 + 2 * twos:2].set(sink + passed)
    return sizes[jax.random.permutation(jax.random.fold_in(stream_key, 2), number_of)]


def normal_values(key, extent, spread, limit, shards=(), kind=jnp.bfloat16):
    level = block_scale(key, extent, shards, -0.22, 0.18) if shards else 1.0
    array = jax.random.normal(key, extent, jnp.float32) * spread * level
    return jnp.minimum(jnp.maximum(array, -limit), limit).astype(kind)


def setup_inputs(seed: int = 0) -> dict:
    seeds = jax.random.split(jax.random.key(seed), 17)
    pol_hidden = normal_values(seeds[0], (TOKENS, D), 1.0, 6.0, ((0, 256),))
    ref_hidden = normal_values(seeds[1], (TOKENS, D), 1.0, 6.0, ((0, 256),))
    pol_mlp_gain = jnp.clip(1.0 + 0.18 * jax.random.normal(seeds[2], (D,), jnp.float32), 0.099609375, 1.8984375).astype(jnp.bfloat16)
    ref_mlp_gain = jnp.clip(1.0 + 0.18 * jax.random.normal(seeds[3], (D,), jnp.float32), 0.099609375, 1.8984375).astype(jnp.bfloat16)
    pol_final_gain = jnp.clip(1.0 + 0.18 * jax.random.normal(seeds[4], (D,), jnp.float32), 0.099609375, 1.8984375).astype(jnp.bfloat16)
    ref_final_gain = jnp.clip(1.0 + 0.18 * jax.random.normal(seeds[5], (D,), jnp.float32), 0.099609375, 1.8984375).astype(jnp.bfloat16)
    pol_gate = normal_values(seeds[6], (D, FF), D ** -0.5, 0.09375, ((1, 64),))
    pol_up = normal_values(seeds[7], (D, FF), D ** -0.5, 0.09375, ((1, 64),))
    pol_down = normal_values(seeds[8], (FF, D), (FF // 4) ** -0.5, 0.109375, ((0, 64),))
    ref_gate = normal_values(seeds[9], (D, FF), D ** -0.5, 0.09375, ((1, 64),))
    ref_up = normal_values(seeds[10], (D, FF), D ** -0.5, 0.09375, ((1, 64),))
    ref_down = normal_values(seeds[11], (FF, D), (FF // 4) ** -0.5, 0.109375, ((0, 64),))
    pol_head = draw_pol_head(jax.random.fold_in(seeds[16], 71), 0)
    ref_head = draw_ref_head(jax.random.fold_in(seeds[16], 71), 0)
    token_ids = with_ends(jax.random.randint(seeds[14], (TOKENS,), 0, V), jax.random.fold_in(seeds[14], 1), 0, V - 1).astype(jnp.int32)
    lengths = uneven_parts(seeds[15], R, TOKENS, LEN_MAX, 2).astype(jnp.int32)
    return {"pol_hidden": pol_hidden, "ref_hidden": ref_hidden, "pol_mlp_gain": pol_mlp_gain, "ref_mlp_gain": ref_mlp_gain, "pol_final_gain": pol_final_gain, "ref_final_gain": ref_final_gain, "pol_gate": pol_gate, "pol_up": pol_up, "pol_down": pol_down, "ref_gate": ref_gate, "ref_up": ref_up, "ref_down": ref_down, "pol_head": pol_head, "ref_head": ref_head, "token_ids": token_ids, "lengths": lengths}


def rms_rows(rows, gain):
    values = rows.astype(jnp.float32)
    scale = lax.rsqrt(lax.optimization_barrier(jnp.mean(values * values, axis=-1, keepdims=True)) + 1e-05)
    return (values * scale * gain.astype(jnp.float32)).astype(jnp.bfloat16)

def sublayer(hidden_in, gain, w_gate, w_up, w_down):
    normed = rms_rows(hidden_in, gain)
    gate = jnp.dot(normed, w_gate, preferred_element_type=jnp.float32)
    upper = jnp.dot(normed, w_up, preferred_element_type=jnp.float32)
    hidden = (jax.nn.silu(gate) * upper).astype(jnp.bfloat16)
    mixed = jnp.dot(hidden, w_down, preferred_element_type=jnp.float32)
    return (hidden_in.astype(jnp.float32) + mixed).astype(jnp.bfloat16)

def log_probs(final, head, token_ids):

    def one_block(pair):
        block_rows, block_targets = pair
        logits = jnp.dot(block_rows, head.T, preferred_element_type=jnp.float32)
        peak = lax.optimization_barrier(jnp.max(logits, axis=1))
        total = lax.optimization_barrier(jnp.sum(jnp.exp(logits - peak[:, None]), axis=1))
        picked = jnp.take_along_axis(logits, block_targets[:, None], axis=1)[:, 0]
        return picked - peak - jnp.log(total)
    return lax.map(one_block, (final.reshape(N_GRP, -1, D), token_ids.reshape(N_GRP, -1))).reshape(-1)

def reference(pol_hidden, ref_hidden, pol_mlp_gain, ref_mlp_gain, pol_final_gain, ref_final_gain, pol_gate, pol_up, pol_down, ref_gate, ref_up, ref_down, pol_head, ref_head, token_ids, lengths):
    pol_out = sublayer(pol_hidden, pol_mlp_gain, pol_gate, pol_up, pol_down)
    ref_out = sublayer(ref_hidden, ref_mlp_gain, ref_gate, ref_up, ref_down)
    pol_logp = log_probs(rms_rows(pol_out, pol_final_gain), pol_head, token_ids)
    ref_logp = log_probs(rms_rows(ref_out, ref_final_gain), ref_head, token_ids)
    ends = jnp.cumsum(lengths).astype(jnp.int32)
    positions = jnp.arange(TOKENS, dtype=jnp.int32)
    owner = lax.optimization_barrier(jnp.sum((positions[:, None] >= ends[None, :]).astype(jnp.int32), axis=1))
    onehot = (owner[:, None] == jnp.arange(R, dtype=jnp.int32)[None, :]).astype(jnp.float32)
    log_ratio = pol_logp - ref_logp
    rollout_ratio = lax.optimization_barrier(jnp.sum(log_ratio[:, None] * onehot, axis=0))
    return (pol_out, ref_out, rollout_ratio)
```

```python
import jax
import jax.numpy as jnp
from jax import lax
from jax.sharding import PartitionSpec as P


def rms_rows(rows, gain):
    values = rows.astype(jnp.float32)
    scale = lax.rsqrt(jnp.mean(values * values, axis=-1, keepdims=True) + 1e-05)
    return (values * scale * gain.astype(jnp.float32)).astype(jnp.bfloat16)


def mlp_partial(piece, gain, w_gate, w_up, w_down):
    normed = rms_rows(piece, gain)
    gate = jnp.dot(normed, w_gate, preferred_element_type=jnp.float32)
    upper = jnp.dot(normed, w_up, preferred_element_type=jnp.float32)
    hidden = (jax.nn.silu(gate) * upper).astype(jnp.bfloat16)
    return jnp.dot(hidden, w_down, preferred_element_type=jnp.float32)


def vocab_terms(token_rows, head_rows, targets, vocab):
    logits = jnp.einsum("td,vd->tv", token_rows, head_rows, preferred_element_type=jnp.float32)
    peak = jnp.max(logits, axis=1)
    total = jnp.sum(jnp.exp(logits - peak[:, None]), axis=1)
    target = jnp.sum(jnp.where(targets[:, None] == vocab[None, :], logits, 0.0), axis=1)
    return (peak, total, target)


def rollout_totals(log_ratio, positions, lengths):
    ends = jnp.cumsum(lengths)
    owner = jnp.sum((positions[:, None] >= ends[None, :]).astype(jnp.int32), axis=1)
    onehot = (owner[:, None] == jnp.arange(lengths.shape[0], dtype=jnp.int32)[None, :]).astype(
        jnp.float32
    )
    return jnp.sum(log_ratio[:, None] * onehot, axis=0)


def per_device(
    pol_hidden,
    ref_hidden,
    pol_mlp_gain,
    ref_mlp_gain,
    pol_final_gain,
    ref_final_gain,
    pol_gate,
    pol_up,
    pol_down,
    ref_gate,
    ref_up,
    ref_down,
    pol_head,
    ref_head,
    token_ids,
    lengths,
):
    rows = pol_hidden.shape[0]
    member = lax.axis_index("mdl")
    group = lax.axis_index("grp")
    members = lax.axis_size("mdl")
    both_in = lax.all_gather(jnp.stack([pol_hidden, ref_hidden]), "mdl", axis=1, tiled=True)
    partials = (
        mlp_partial(both_in[0], pol_mlp_gain, pol_gate, pol_up, pol_down),
        mlp_partial(both_in[1], ref_mlp_gain, ref_gate, ref_up, ref_down),
    )
    mixed = lax.psum(partials, "mdl")
    outs = [(both_in[i].astype(jnp.float32) + mixed[i]).astype(jnp.bfloat16) for i in range(2)]
    finals = jnp.stack([rms_rows(outs[0], pol_final_gain), rms_rows(outs[1], ref_final_gain)])
    own = [lax.dynamic_slice_in_dim(o, member * rows, rows, axis=0) for o in outs]
    every = lax.all_gather(finals, "grp", axis=1, tiled=True)
    voc_dev = pol_head.shape[0]
    positions = jnp.arange(every.shape[1], dtype=jnp.int32)
    vocab = (group * members + member) * voc_dev + jnp.arange(voc_dev, dtype=jnp.int32)
    pol_terms = vocab_terms(every[0], pol_head, token_ids, vocab)
    ref_terms = vocab_terms(every[1], ref_head, token_ids, vocab)
    peaks = lax.pmax(lax.pmax((pol_terms[0], ref_terms[0]), "mdl"), "grp")
    sums = lax.psum(
        lax.psum(
            (
                pol_terms[1] * jnp.exp(pol_terms[0] - peaks[0]),
                pol_terms[2],
                ref_terms[1] * jnp.exp(ref_terms[0] - peaks[1]),
                ref_terms[2],
            ),
            "mdl",
        ),
        "grp",
    )
    pol_logp = sums[1] - peaks[0] - jnp.log(sums[0])
    ref_logp = sums[3] - peaks[1] - jnp.log(sums[2])
    rollout_ratio = rollout_totals(pol_logp - ref_logp, positions, lengths)
    return (own[0], own[1], rollout_ratio)


def solution(mesh):
    placed = (
        P(("grp", "mdl"), None),
        P(("grp", "mdl"), None),
        P(),
        P(),
        P(),
        P(),
        P(None, "mdl"),
        P(None, "mdl"),
        P("mdl", None),
        P(None, "mdl"),
        P(None, "mdl"),
        P("mdl", None),
        P(("grp", "mdl"), None),
        P(("grp", "mdl"), None),
        P(),
        P(),
    )
    return jax.shard_map(
        per_device,
        mesh=mesh,
        in_specs=placed,
        out_specs=(P(("grp", "mdl"), None), P(("grp", "mdl"), None), P()),
        check_vma=False,
    )
```

```python
import jax
import jax.numpy as jnp
from jax import lax
from jax.sharding import PartitionSpec as P


def rms_rows(rows, gain):
    values = rows.astype(jnp.float32)
    scale = lax.rsqrt(jnp.mean(values * values, axis=-1, keepdims=True) + 1e-05)
    return (values * scale * gain.astype(jnp.float32)).astype(jnp.bfloat16)


def mlp_partial(piece, gain, w_gate, w_up, w_down):
    normed = rms_rows(piece, gain)
    gate = jnp.dot(normed, w_gate, preferred_element_type=jnp.float32)
    upper = jnp.dot(normed, w_up, preferred_element_type=jnp.float32)
    hidden = (jax.nn.silu(gate) * upper).astype(jnp.bfloat16)
    return jnp.dot(hidden, w_down, preferred_element_type=jnp.float32)


def vocab_terms(token_rows, head_rows, targets, vocab):
    logits = jnp.einsum("td,vd->tv", token_rows, head_rows, preferred_element_type=jnp.float32)
    peak = jnp.max(logits, axis=1)
    total = jnp.sum(jnp.exp(logits - peak[:, None]), axis=1)
    target = jnp.sum(jnp.where(targets[:, None] == vocab[None, :], logits, 0.0), axis=1)
    return (peak, total, target)


def merge_terms(lo, hi):
    peak = jnp.maximum(lo[:, 0], hi[:, 0])
    total = lo[:, 1] * jnp.exp(lo[:, 0] - peak) + hi[:, 1] * jnp.exp(hi[:, 0] - peak)
    return jnp.stack([peak, total, lo[:, 2] + hi[:, 2]], axis=1)


def rollout_totals(log_ratio, positions, lengths):
    ends = jnp.cumsum(lengths)
    owner = jnp.sum((positions[:, None] >= ends[None, :]).astype(jnp.int32), axis=1)
    onehot = (owner[:, None] == jnp.arange(lengths.shape[0], dtype=jnp.int32)[None, :]).astype(
        jnp.float32
    )
    return jnp.sum(log_ratio[:, None] * onehot, axis=0)


def per_device(
    pol_hidden,
    ref_hidden,
    pol_mlp_gain,
    ref_mlp_gain,
    pol_final_gain,
    ref_final_gain,
    pol_gate,
    pol_up,
    pol_down,
    ref_gate,
    ref_up,
    ref_down,
    pol_head,
    ref_head,
    token_ids,
    lengths,
):
    rows = pol_hidden.shape[0]
    member = lax.axis_index("mdl")
    group = lax.axis_index("grp")
    members = lax.axis_size("mdl")
    both_in = lax.all_gather(jnp.stack([pol_hidden, ref_hidden]), "mdl", axis=1, tiled=True)
    partials = (
        mlp_partial(both_in[0], pol_mlp_gain, pol_gate, pol_up, pol_down),
        mlp_partial(both_in[1], ref_mlp_gain, ref_gate, ref_up, ref_down),
    )
    mixed = lax.psum(partials, "mdl")
    outs = [(both_in[i].astype(jnp.float32) + mixed[i]).astype(jnp.bfloat16) for i in range(2)]
    finals = (rms_rows(outs[0], pol_final_gain), rms_rows(outs[1], ref_final_gain))
    own = [lax.dynamic_slice_in_dim(o, member * rows, rows, axis=0) for o in outs]
    first = (member % 2) == 0
    chosen = jnp.where(first, finals[0], finals[1])
    every = lax.all_gather(chosen, "grp", axis=0, tiled=True)
    pair = [(i, i ^ 1) for i in range(members)]
    mine = jnp.where(first, pol_head, ref_head)
    theirs = lax.ppermute(jnp.where(first, ref_head, pol_head), "mdl", pair)
    voc_dev = pol_head.shape[0]
    positions = jnp.arange(every.shape[0], dtype=jnp.int32)
    base = group * members
    vocab = jnp.concatenate(
        [
            (base + member) * voc_dev + jnp.arange(voc_dev, dtype=jnp.int32),
            (base + (member ^ 1)) * voc_dev + jnp.arange(voc_dev, dtype=jnp.int32),
        ]
    )
    own_terms = jnp.stack(vocab_terms(every, jnp.concatenate([mine, theirs]), token_ids, vocab))
    other_terms = lax.ppermute(own_terms, "mdl", pair)
    state = jnp.where(first, jnp.stack([own_terms, other_terms]), jnp.stack([other_terms, own_terms]))
    rounds = [("mdl", 2), ("mdl", 4), ("mdl", 8), ("mdl", 16), ("mdl", 32), ("grp", 1), ("grp", 2)]
    for axis, bit in rounds:
        size = lax.axis_size(axis)
        other = lax.ppermute(state, axis, [(i, i ^ bit) for i in range(size)])
        low = (lax.axis_index(axis) & bit) == 0
        state = merge_terms(jnp.where(low, state, other), jnp.where(low, other, state))
    logp = state[:, 2] - state[:, 0] - jnp.log(state[:, 1])
    rollout_ratio = rollout_totals(logp[0] - logp[1], positions, lengths)
    return (own[0], own[1], rollout_ratio)


def solution(mesh):
    placed = (
        P(("grp", "mdl"), None),
        P(("grp", "mdl"), None),
        P(),
        P(),
        P(),
        P(),
        P(None, "mdl"),
        P(None, "mdl"),
        P("mdl", None),
        P(None, "mdl"),
        P(None, "mdl"),
        P("mdl", None),
        P(("grp", "mdl"), None),
        P(("grp", "mdl"), None),
        P(),
        P(),
    )
    return jax.shard_map(
        per_device,
        mesh=mesh,
        in_specs=placed,
        out_specs=(P(("grp", "mdl"), None), P(("grp", "mdl"), None), P()),
        check_vma=False,
    )
```

```python
import jax
import jax.numpy as jnp
from jax import lax
from jax.sharding import Mesh
from jax.sharding import PartitionSpec as P

SWAP = [(0, 1), (1, 0)]


def rms_rows(rows, gain):
    values = rows.astype(jnp.float32)
    scale = lax.rsqrt(jnp.mean(values * values, axis=-1, keepdims=True) + 1e-05)
    return (values * scale * gain.astype(jnp.float32)).astype(jnp.bfloat16)


def mlp_partial(piece, gain, w_gate, w_up, w_down):
    normed = rms_rows(piece, gain)
    gate = jnp.dot(normed, w_gate, preferred_element_type=jnp.float32)
    upper = jnp.dot(normed, w_up, preferred_element_type=jnp.float32)
    hidden = (jax.nn.silu(gate) * upper).astype(jnp.bfloat16)
    return jnp.dot(hidden, w_down, preferred_element_type=jnp.float32)


def vocab_terms(token_rows, head_rows, targets, vocab):
    logits = jnp.einsum("td,vd->tv", token_rows, head_rows, preferred_element_type=jnp.float32)
    peak = jnp.max(logits, axis=1)
    total = jnp.sum(jnp.exp(logits - peak[:, None]), axis=1)
    target = jnp.sum(jnp.where(targets[:, None] == vocab[None, :], logits, 0.0), axis=1)
    return (peak, total, target)


def merge_terms(lo, hi):
    peak = jnp.maximum(lo[:, 0], hi[:, 0])
    total = lo[:, 1] * jnp.exp(lo[:, 0] - peak) + hi[:, 1] * jnp.exp(hi[:, 0] - peak)
    return jnp.stack([peak, total, lo[:, 2] + hi[:, 2]], axis=1)


def rollout_totals(log_ratio, positions, lengths):
    ends = jnp.cumsum(lengths)
    owner = jnp.sum((positions[:, None] >= ends[None, :]).astype(jnp.int32), axis=1)
    onehot = (owner[:, None] == jnp.arange(lengths.shape[0], dtype=jnp.int32)[None, :]).astype(
        jnp.float32
    )
    return jnp.sum(log_ratio[:, None] * onehot, axis=0)


def pick(first, pol, ref):
    return jnp.where(first, pol, ref), jnp.where(first, ref, pol)


def per_device(
    pol_hidden,
    ref_hidden,
    pol_mlp_gain,
    ref_mlp_gain,
    pol_final_gain,
    ref_final_gain,
    pol_gate,
    pol_up,
    pol_down,
    ref_gate,
    ref_up,
    ref_down,
    pol_head,
    ref_head,
    token_ids,
    lengths,
):
    rows = pol_hidden.shape[0]
    core = lax.axis_index("core")
    spot = lax.axis_index("zx")
    group = lax.axis_index("grp")
    first = core == 0
    per_group = lax.axis_size("zx") * 2
    member = spot * 2 + core
    partner = spot * 2 + (1 - core)

    keep_w, give_w = pick(first, jnp.stack([pol_gate, pol_up]), jnp.stack([ref_gate, ref_up]))
    keep_d, give_d = pick(first, pol_down, ref_down)
    got_w = lax.ppermute(give_w, "core", SWAP)
    got_d = lax.ppermute(give_d, "core", SWAP)
    keep_h, give_h = pick(first, pol_hidden, ref_hidden)
    got_h = lax.ppermute(give_h, "core", SWAP)
    pair_rows = jnp.where(
        first, jnp.concatenate([keep_h, got_h]), jnp.concatenate([got_h, keep_h])
    )
    group_rows = lax.all_gather(pair_rows, "zx", axis=0, tiled=True)
    mlp_gain = jnp.where(first, pol_mlp_gain, ref_mlp_gain)
    partial = mlp_partial(group_rows, mlp_gain, keep_w[0], keep_w[1], keep_d) + mlp_partial(
        group_rows, mlp_gain, got_w[0], got_w[1], got_d
    )
    mixed = lax.psum(partial, "zx")
    out = (group_rows.astype(jnp.float32) + mixed).astype(jnp.bfloat16)
    final = rms_rows(out, jnp.where(first, pol_final_gain, ref_final_gain))
    mine_out = lax.dynamic_slice_in_dim(out, member * rows, rows, axis=0)
    sent_out = lax.ppermute(lax.dynamic_slice_in_dim(out, partner * rows, rows, axis=0), "core", SWAP)
    pol_out = jnp.where(first, mine_out, sent_out)
    ref_out = jnp.where(first, sent_out, mine_out)

    every = lax.all_gather(final, "grp", axis=0, tiled=True)
    keep_v, give_v = pick(first, pol_head, ref_head)
    got_v = lax.ppermute(give_v, "core", SWAP)
    voc_dev = pol_head.shape[0]
    positions = jnp.arange(every.shape[0], dtype=jnp.int32)
    base = group * per_group
    vocab = jnp.concatenate(
        [
            (base + member) * voc_dev + jnp.arange(voc_dev, dtype=jnp.int32),
            (base + partner) * voc_dev + jnp.arange(voc_dev, dtype=jnp.int32),
        ]
    )
    own_terms = jnp.stack(vocab_terms(every, jnp.concatenate([keep_v, got_v]), token_ids, vocab))
    other_terms = lax.ppermute(own_terms, "core", SWAP)
    state = jnp.where(first, jnp.stack([own_terms, other_terms]), jnp.stack([other_terms, own_terms]))
    rounds = [("zx", 1), ("zx", 2), ("zx", 4), ("zx", 8), ("zx", 16), ("grp", 1), ("grp", 2)]
    for axis, bit in rounds:
        size = lax.axis_size(axis)
        other = lax.ppermute(state, axis, [(i, i ^ bit) for i in range(size)])
        low = (lax.axis_index(axis) & bit) == 0
        state = merge_terms(jnp.where(low, state, other), jnp.where(low, other, state))
    logp = state[:, 2] - state[:, 0] - jnp.log(state[:, 1])
    rollout_ratio = rollout_totals(logp[0] - logp[1], positions, lengths)
    return (pol_out, ref_out, rollout_ratio)


def solution(mesh):
    groups, members = mesh.devices.shape
    split = Mesh(mesh.devices.reshape(groups, members // 2, 2), ("grp", "zx", "core"))
    rows = P(("grp", "zx", "core"), None)
    units = ("zx", "core")
    placed = (
        rows,
        rows,
        P(),
        P(),
        P(),
        P(),
        P(None, units),
        P(None, units),
        P(units, None),
        P(None, units),
        P(None, units),
        P(units, None),
        rows,
        rows,
        P(),
        P(),
    )
    return jax.shard_map(
        per_device,
        mesh=split,
        in_specs=placed,
        out_specs=(rows, rows, P()),
        check_vma=False,
    )
```

```python
import jax
import jax.numpy as jnp
from jax import lax
from jax.sharding import Mesh
from jax.sharding import PartitionSpec as P

SWAP = [(0, 1), (1, 0)]


def rms_rows(rows, gain):
    values = rows.astype(jnp.float32)
    scale = lax.rsqrt(jnp.mean(values * values, axis=-1, keepdims=True) + 1e-05)
    return (values * scale * gain.astype(jnp.float32)).astype(jnp.bfloat16)


def mlp_partial(piece, gain, w_gate, w_up, w_down):
    normed = rms_rows(piece, gain)
    gate = jnp.dot(normed, w_gate, preferred_element_type=jnp.float32)
    upper = jnp.dot(normed, w_up, preferred_element_type=jnp.float32)
    hidden = (jax.nn.silu(gate) * upper).astype(jnp.bfloat16)
    return jnp.dot(hidden, w_down, preferred_element_type=jnp.float32)


def vocab_terms(token_rows, head_rows, targets, vocab):
    logits = jnp.einsum("td,vd->tv", token_rows, head_rows, preferred_element_type=jnp.float32)
    peak = jnp.max(logits, axis=1)
    total = jnp.sum(jnp.exp(logits - peak[:, None]), axis=1)
    target = jnp.sum(jnp.where(targets[:, None] == vocab[None, :], logits, 0.0), axis=1)
    return (peak, total, target)


def merge_terms(lo, hi):
    peak = jnp.maximum(lo[:, 0], hi[:, 0])
    total = lo[:, 1] * jnp.exp(lo[:, 0] - peak) + hi[:, 1] * jnp.exp(hi[:, 0] - peak)
    return jnp.stack([peak, total, lo[:, 2] + hi[:, 2]], axis=1)


def rollout_totals(log_ratio, positions, lengths):
    ends = jnp.cumsum(lengths)
    owner = jnp.sum((positions[:, None] >= ends[None, :]).astype(jnp.int32), axis=1)
    onehot = (owner[:, None] == jnp.arange(lengths.shape[0], dtype=jnp.int32)[None, :]).astype(
        jnp.float32
    )
    return jnp.sum(log_ratio[:, None] * onehot, axis=0)


def zx_bits():
    size = lax.axis_size("zx")
    return [1 << k for k in reversed(range(size.bit_length() - 1))]


def gather_doubling(block):
    bits = zx_bits()
    spot = lax.axis_index("zx")
    held = block.reshape((1,) * len(bits) + block.shape)
    for bit in [16, 8, 2, 4, 1]:
        if bit not in bits:
            continue
        dim = bits.index(bit)
        other = lax.ppermute(held, "zx", [(i, i ^ bit) for i in range(lax.axis_size("zx"))])
        low = (spot & bit) == 0
        held = jnp.concatenate([jnp.where(low, held, other), jnp.where(low, other, held)], axis=dim)
    return held.reshape((-1,) + block.shape[1:])


def scatter_halving(full):
    bits = zx_bits()
    spot = lax.axis_index("zx")
    held = full.reshape((2,) * len(bits) + (-1,) + full.shape[1:])
    for bit in [1, 4, 2, 8, 16]:
        if bit not in bits:
            continue
        dim = bits.index(bit)
        lower = lax.slice_in_dim(held, 0, 1, axis=dim)
        upper = lax.slice_in_dim(held, 1, 2, axis=dim)
        low = (spot & bit) == 0
        other = lax.ppermute(
            jnp.where(low, upper, lower), "zx", [(i, i ^ bit) for i in range(lax.axis_size("zx"))]
        )
        held = jnp.where(low, lower, upper) + other
    return held.reshape((-1,) + full.shape[1:])


def pick(first, pol, ref):
    return jnp.where(first, pol, ref), jnp.where(first, ref, pol)


def per_device(
    pol_hidden,
    ref_hidden,
    pol_mlp_gain,
    ref_mlp_gain,
    pol_final_gain,
    ref_final_gain,
    pol_gate,
    pol_up,
    pol_down,
    ref_gate,
    ref_up,
    ref_down,
    pol_head,
    ref_head,
    token_ids,
    lengths,
):
    rows = pol_hidden.shape[0]
    core = lax.axis_index("core")
    spot = lax.axis_index("zx")
    group = lax.axis_index("grp")
    first = core == 0
    per_group = lax.axis_size("zx") * 2
    member = spot * 2 + core
    partner = spot * 2 + (1 - core)

    keep_w, give_w = pick(first, jnp.stack([pol_gate, pol_up]), jnp.stack([ref_gate, ref_up]))
    keep_d, give_d = pick(first, pol_down, ref_down)
    got_w = lax.ppermute(give_w, "core", SWAP)
    got_d = lax.ppermute(give_d, "core", SWAP)
    keep_h, give_h = pick(first, pol_hidden, ref_hidden)
    got_h = lax.ppermute(give_h, "core", SWAP)
    pair_rows = jnp.where(
        first, jnp.concatenate([keep_h, got_h]), jnp.concatenate([got_h, keep_h])
    )
    group_rows = gather_doubling(pair_rows)
    mlp_gain = jnp.where(first, pol_mlp_gain, ref_mlp_gain)
    partial = mlp_partial(group_rows, mlp_gain, keep_w[0], keep_w[1], keep_d) + mlp_partial(
        group_rows, mlp_gain, got_w[0], got_w[1], got_d
    )
    mixed = scatter_halving(partial)
    out = (pair_rows.astype(jnp.float32) + mixed).astype(jnp.bfloat16)
    final = gather_doubling(rms_rows(out, jnp.where(first, pol_final_gain, ref_final_gain)))
    mine_out = lax.dynamic_slice_in_dim(out, core * rows, rows, axis=0)
    sent_out = lax.ppermute(lax.dynamic_slice_in_dim(out, (1 - core) * rows, rows, axis=0), "core", SWAP)
    pol_out = jnp.where(first, mine_out, sent_out)
    ref_out = jnp.where(first, sent_out, mine_out)

    every = lax.all_gather(final, "grp", axis=0, tiled=True)
    keep_v, give_v = pick(first, pol_head, ref_head)
    got_v = lax.ppermute(give_v, "core", SWAP)
    voc_dev = pol_head.shape[0]
    positions = jnp.arange(every.shape[0], dtype=jnp.int32)
    base = group * per_group
    vocab = jnp.concatenate(
        [
            (base + member) * voc_dev + jnp.arange(voc_dev, dtype=jnp.int32),
            (base + partner) * voc_dev + jnp.arange(voc_dev, dtype=jnp.int32),
        ]
    )
    own_terms = jnp.stack(vocab_terms(every, jnp.concatenate([keep_v, got_v]), token_ids, vocab))
    other_terms = lax.ppermute(own_terms, "core", SWAP)
    state = jnp.where(first, jnp.stack([own_terms, other_terms]), jnp.stack([other_terms, own_terms]))
    rounds = [("zx", 1), ("zx", 2), ("zx", 4), ("zx", 8), ("zx", 16), ("grp", 1), ("grp", 2)]
    for axis, bit in rounds:
        size = lax.axis_size(axis)
        other = lax.ppermute(state, axis, [(i, i ^ bit) for i in range(size)])
        low = (lax.axis_index(axis) & bit) == 0
        state = merge_terms(jnp.where(low, state, other), jnp.where(low, other, state))
    logp = state[:, 2] - state[:, 0] - jnp.log(state[:, 1])
    rollout_ratio = rollout_totals(logp[0] - logp[1], positions, lengths)
    return (pol_out, ref_out, rollout_ratio)


def solution(mesh):
    groups, members = mesh.devices.shape
    split = Mesh(mesh.devices.reshape(groups, members // 2, 2), ("grp", "zx", "core"))
    rows = P(("grp", "zx", "core"), None)
    units = ("zx", "core")
    placed = (
        rows,
        rows,
        P(),
        P(),
        P(),
        P(),
        P(None, units),
        P(None, units),
        P(units, None),
        P(None, units),
        P(None, units),
        P(units, None),
        rows,
        rows,
        P(),
        P(),
    )
    return jax.shard_map(
        per_device,
        mesh=split,
        in_specs=placed,
        out_specs=(rows, rows, P()),
        check_vma=False,
    )
```

```python
import jax
import jax.numpy as jnp
from jax import lax
from jax.sharding import Mesh
from jax.sharding import PartitionSpec as P

SWAP = [(0, 1), (1, 0)]


def rms_rows(rows, gain):
    values = rows.astype(jnp.float32)
    scale = lax.rsqrt(jnp.mean(values * values, axis=-1, keepdims=True) + 1e-05)
    return (values * scale * gain.astype(jnp.float32)).astype(jnp.bfloat16)


def mlp_partial(piece, gain, w_gate, w_up, w_down):
    normed = rms_rows(piece, gain)
    gate = jnp.dot(normed, w_gate, preferred_element_type=jnp.float32)
    upper = jnp.dot(normed, w_up, preferred_element_type=jnp.float32)
    hidden = (jax.nn.silu(gate) * upper).astype(jnp.bfloat16)
    return jnp.dot(hidden, w_down, preferred_element_type=jnp.float32)


def vocab_terms(token_rows, head_rows, targets, vocab):
    logits = jnp.einsum("td,vd->tv", token_rows, head_rows, preferred_element_type=jnp.float32)
    peak = jnp.max(logits, axis=1)
    total = jnp.sum(jnp.exp(logits - peak[:, None]), axis=1)
    target = jnp.sum(jnp.where(targets[:, None] == vocab[None, :], logits, 0.0), axis=1)
    return (peak, total, target)


def merge_terms(lo, hi):
    peak = jnp.maximum(lo[:, 0], hi[:, 0])
    total = lo[:, 1] * jnp.exp(lo[:, 0] - peak) + hi[:, 1] * jnp.exp(hi[:, 0] - peak)
    return jnp.stack([peak, total, lo[:, 2] + hi[:, 2]], axis=1)


def rollout_totals(log_ratio, positions, lengths):
    ends = jnp.cumsum(lengths)
    owner = jnp.sum((positions[:, None] >= ends[None, :]).astype(jnp.int32), axis=1)
    onehot = (owner[:, None] == jnp.arange(lengths.shape[0], dtype=jnp.int32)[None, :]).astype(
        jnp.float32
    )
    return jnp.sum(log_ratio[:, None] * onehot, axis=0)


def zx_bits():
    size = lax.axis_size("zx")
    return [1 << k for k in reversed(range(size.bit_length() - 1))]


def gather_doubling(block, orders=((16, 8, 2, 4, 1), (16, 2, 8, 1, 4))):
    bits = zx_bits()
    spot = lax.axis_index("zx")
    size = lax.axis_size("zx")
    width = block.shape[-1] // len(orders)
    parts = []
    for k in range(len(orders)):
        piece = lax.slice_in_dim(block, k * width, (k + 1) * width, axis=block.ndim - 1)
        parts.append(piece.reshape((1,) * len(bits) + piece.shape))
    for step in range(len(orders[0])):
        for k, order in enumerate(orders):
            bit = order[step]
            if bit not in bits:
                continue
            dim = bits.index(bit)
            held = parts[k]
            other = lax.ppermute(held, "zx", [(i, i ^ bit) for i in range(size)])
            low = (spot & bit) == 0
            parts[k] = jnp.concatenate(
                [jnp.where(low, held, other), jnp.where(low, other, held)], axis=dim
            )
    rows = [p.reshape((-1,) + p.shape[len(bits) + 1 :]) for p in parts]
    return jnp.concatenate(rows, axis=-1)


def scatter_halving(full, orders=((1, 4, 2, 8, 16), (4, 1, 8, 2, 16))):
    bits = zx_bits()
    spot = lax.axis_index("zx")
    size = lax.axis_size("zx")
    width = full.shape[-1] // len(orders)
    parts = []
    for k in range(len(orders)):
        piece = lax.slice_in_dim(full, k * width, (k + 1) * width, axis=full.ndim - 1)
        parts.append(piece.reshape((2,) * len(bits) + (-1,) + piece.shape[1:]))
    for step in range(len(orders[0])):
        for k, order in enumerate(orders):
            bit = order[step]
            if bit not in bits:
                continue
            dim = bits.index(bit)
            held = parts[k]
            lower = lax.slice_in_dim(held, 0, 1, axis=dim)
            upper = lax.slice_in_dim(held, 1, 2, axis=dim)
            low = (spot & bit) == 0
            other = lax.ppermute(
                jnp.where(low, upper, lower), "zx", [(i, i ^ bit) for i in range(size)]
            )
            parts[k] = jnp.where(low, lower, upper) + other
    rows = [p.reshape((-1,) + full.shape[1:-1] + (width,)) for p in parts]
    return jnp.concatenate(rows, axis=-1)


def pick(first, pol, ref):
    return jnp.where(first, pol, ref), jnp.where(first, ref, pol)


def per_device(
    pol_hidden,
    ref_hidden,
    pol_mlp_gain,
    ref_mlp_gain,
    pol_final_gain,
    ref_final_gain,
    pol_gate,
    pol_up,
    pol_down,
    ref_gate,
    ref_up,
    ref_down,
    pol_head,
    ref_head,
    token_ids,
    lengths,
):
    rows = pol_hidden.shape[0]
    core = lax.axis_index("core")
    spot = lax.axis_index("zx")
    group = lax.axis_index("grp")
    first = core == 0
    per_group = lax.axis_size("zx") * 2
    member = spot * 2 + core
    partner = spot * 2 + (1 - core)

    keep_w, give_w = pick(first, jnp.stack([pol_gate, pol_up]), jnp.stack([ref_gate, ref_up]))
    keep_d, give_d = pick(first, pol_down, ref_down)
    got_w = lax.ppermute(give_w, "core", SWAP)
    got_d = lax.ppermute(give_d, "core", SWAP)
    keep_h, give_h = pick(first, pol_hidden, ref_hidden)
    got_h = lax.ppermute(give_h, "core", SWAP)
    pair_rows = jnp.where(
        first, jnp.concatenate([keep_h, got_h]), jnp.concatenate([got_h, keep_h])
    )
    group_rows = gather_doubling(pair_rows)
    mlp_gain = jnp.where(first, pol_mlp_gain, ref_mlp_gain)
    partial = mlp_partial(group_rows, mlp_gain, keep_w[0], keep_w[1], keep_d) + mlp_partial(
        group_rows, mlp_gain, got_w[0], got_w[1], got_d
    )
    mixed = scatter_halving(partial)
    out = (pair_rows.astype(jnp.float32) + mixed).astype(jnp.bfloat16)
    final = gather_doubling(rms_rows(out, jnp.where(first, pol_final_gain, ref_final_gain)))
    mine_out = lax.dynamic_slice_in_dim(out, core * rows, rows, axis=0)
    sent_out = lax.ppermute(lax.dynamic_slice_in_dim(out, (1 - core) * rows, rows, axis=0), "core", SWAP)
    pol_out = jnp.where(first, mine_out, sent_out)
    ref_out = jnp.where(first, sent_out, mine_out)

    every = lax.all_gather(final, "grp", axis=0, tiled=True)
    keep_v, give_v = pick(first, pol_head, ref_head)
    got_v = lax.ppermute(give_v, "core", SWAP)
    voc_dev = pol_head.shape[0]
    positions = jnp.arange(every.shape[0], dtype=jnp.int32)
    base = group * per_group
    vocab = jnp.concatenate(
        [
            (base + member) * voc_dev + jnp.arange(voc_dev, dtype=jnp.int32),
            (base + partner) * voc_dev + jnp.arange(voc_dev, dtype=jnp.int32),
        ]
    )
    own_terms = jnp.stack(vocab_terms(every, jnp.concatenate([keep_v, got_v]), token_ids, vocab))
    other_terms = lax.ppermute(own_terms, "core", SWAP)
    state = jnp.where(first, jnp.stack([own_terms, other_terms]), jnp.stack([other_terms, own_terms]))
    rounds = [("zx", 1), ("zx", 2), ("zx", 4), ("zx", 8), ("zx", 16), ("grp", 1), ("grp", 2)]
    for axis, bit in rounds:
        size = lax.axis_size(axis)
        other = lax.ppermute(state, axis, [(i, i ^ bit) for i in range(size)])
        low = (lax.axis_index(axis) & bit) == 0
        state = merge_terms(jnp.where(low, state, other), jnp.where(low, other, state))
    logp = state[:, 2] - state[:, 0] - jnp.log(state[:, 1])
    rollout_ratio = rollout_totals(logp[0] - logp[1], positions, lengths)
    return (pol_out, ref_out, rollout_ratio)


def solution(mesh):
    groups, members = mesh.devices.shape
    split = Mesh(mesh.devices.reshape(groups, members // 2, 2), ("grp", "zx", "core"))
    rows = P(("grp", "zx", "core"), None)
    units = ("zx", "core")
    placed = (
        rows,
        rows,
        P(),
        P(),
        P(),
        P(),
        P(None, units),
        P(None, units),
        P(units, None),
        P(None, units),
        P(None, units),
        P(units, None),
        rows,
        rows,
        P(),
        P(),
    )
    return jax.shard_map(
        per_device,
        mesh=split,
        in_specs=placed,
        out_specs=(rows, rows, P()),
        check_vma=False,
    )
```

```python
import jax
import jax.numpy as jnp
from jax import lax
from jax.sharding import Mesh
from jax.sharding import PartitionSpec as P

SWAP = [(0, 1), (1, 0)]


def rms_rows(rows, gain):
    values = rows.astype(jnp.float32)
    scale = lax.rsqrt(jnp.mean(values * values, axis=-1, keepdims=True) + 1e-05)
    return (values * scale * gain.astype(jnp.float32)).astype(jnp.bfloat16)


def mlp_partial(piece, gain, w_gate, w_up, w_down):
    normed = rms_rows(piece, gain)
    gate = jnp.dot(normed, w_gate, preferred_element_type=jnp.float32)
    upper = jnp.dot(normed, w_up, preferred_element_type=jnp.float32)
    hidden = (jax.nn.silu(gate) * upper).astype(jnp.bfloat16)
    return jnp.dot(hidden, w_down, preferred_element_type=jnp.float32)


def vocab_terms(token_rows, head_rows, targets, vocab):
    logits = jnp.einsum("td,vd->tv", token_rows, head_rows, preferred_element_type=jnp.float32)
    peak = jnp.max(logits, axis=1)
    total = jnp.sum(jnp.exp(logits - peak[:, None]), axis=1)
    target = jnp.sum(jnp.where(targets[:, None] == vocab[None, :], logits, 0.0), axis=1)
    return (peak, total, target)


def merge_terms(lo, hi):
    peak = jnp.maximum(lo[:, 0], hi[:, 0])
    total = lo[:, 1] * jnp.exp(lo[:, 0] - peak) + hi[:, 1] * jnp.exp(hi[:, 0] - peak)
    return jnp.stack([peak, total, lo[:, 2] + hi[:, 2]], axis=1)


def exchange_merge(state, axis, span, stride):
    index = lax.axis_index(axis)
    size = lax.axis_size(axis)
    digit = (index // stride) % span
    got = [state]
    for shift in range(1, span):
        got.append(lax.ppermute(state, axis, [(i, i ^ (shift * stride)) for i in range(size)]))
    canon = jnp.stack(got)[jnp.arange(span, dtype=jnp.int32) ^ digit]
    parts = [canon[j] for j in range(span)]
    while len(parts) > 1:
        parts = [merge_terms(parts[k], parts[k + 1]) for k in range(0, len(parts), 2)]
    return parts[0]


def rollout_totals(log_ratio, positions, lengths):
    ends = jnp.cumsum(lengths)
    owner = jnp.sum((positions[:, None] >= ends[None, :]).astype(jnp.int32), axis=1)
    onehot = (owner[:, None] == jnp.arange(lengths.shape[0], dtype=jnp.int32)[None, :]).astype(
        jnp.float32
    )
    return jnp.sum(log_ratio[:, None] * onehot, axis=0)


def zx_bits():
    size = lax.axis_size("zx")
    return [1 << k for k in reversed(range(size.bit_length() - 1))]


def gather_doubling(block, orders=((16, 8, 2, 4, 1), (16, 2, 8, 1, 4)), hold=None):
    bits = zx_bits()
    spot = lax.axis_index("zx")
    size = lax.axis_size("zx")
    width = block.shape[-1] // len(orders)
    parts = []
    for k in range(len(orders)):
        piece = lax.slice_in_dim(block, k * width, (k + 1) * width, axis=block.ndim - 1)
        parts.append(piece.reshape((1,) * len(bits) + piece.shape))
    for step in range(len(orders[0])):
        for k, order in enumerate(orders):
            bit = order[step]
            if bit not in bits:
                continue
            dim = bits.index(bit)
            held = parts[k]
            other = lax.ppermute(held, "zx", [(i, i ^ bit) for i in range(size)])
            low = (spot & bit) == 0
            parts[k] = jnp.concatenate(
                [jnp.where(low, held, other), jnp.where(low, other, held)], axis=dim
            )
        if step == 0 and hold is not None:
            parts, hold = lax.optimization_barrier((parts, hold))
    rows = [p.reshape((-1,) + p.shape[len(bits) + 1 :]) for p in parts]
    if hold is None:
        return jnp.concatenate(rows, axis=-1)
    return jnp.concatenate(rows, axis=-1), hold


def scatter_halving(full, orders=((1, 4, 2, 8, 16), (4, 1, 8, 2, 16))):
    bits = zx_bits()
    spot = lax.axis_index("zx")
    size = lax.axis_size("zx")
    width = full.shape[-1] // len(orders)
    parts = []
    for k in range(len(orders)):
        piece = lax.slice_in_dim(full, k * width, (k + 1) * width, axis=full.ndim - 1)
        parts.append(piece.reshape((2,) * len(bits) + (-1,) + piece.shape[1:]))
    for step in range(len(orders[0])):
        for k, order in enumerate(orders):
            bit = order[step]
            if bit not in bits:
                continue
            dim = bits.index(bit)
            held = parts[k]
            lower = lax.slice_in_dim(held, 0, 1, axis=dim)
            upper = lax.slice_in_dim(held, 1, 2, axis=dim)
            low = (spot & bit) == 0
            other = lax.ppermute(
                jnp.where(low, upper, lower), "zx", [(i, i ^ bit) for i in range(size)]
            )
            parts[k] = jnp.where(low, lower, upper) + other
    rows = [p.reshape((-1,) + full.shape[1:-1] + (width,)) for p in parts]
    return jnp.concatenate(rows, axis=-1)


def pick(first, pol, ref):
    return jnp.where(first, pol, ref), jnp.where(first, ref, pol)


def per_device(
    pol_hidden,
    ref_hidden,
    pol_mlp_gain,
    ref_mlp_gain,
    pol_final_gain,
    ref_final_gain,
    pol_gate,
    pol_up,
    pol_down,
    ref_gate,
    ref_up,
    ref_down,
    pol_head,
    ref_head,
    token_ids,
    lengths,
):
    rows = pol_hidden.shape[0]
    core = lax.axis_index("core")
    spot = lax.axis_index("zx")
    group = lax.axis_index("grp")
    first = core == 0
    per_group = lax.axis_size("zx") * 2
    member = spot * 2 + core
    partner = spot * 2 + (1 - core)

    keep_h, give_h = pick(first, pol_hidden, ref_hidden)
    got_h = lax.ppermute(give_h, "core", SWAP)
    pair_rows = jnp.where(
        first, jnp.concatenate([keep_h, got_h]), jnp.concatenate([got_h, keep_h])
    )
    weights = (pol_gate, pol_up, pol_down, ref_gate, ref_up, ref_down)
    group_rows, weights = gather_doubling(pair_rows, hold=weights)
    pol_gate, pol_up, pol_down, ref_gate, ref_up, ref_down = weights
    keep_w, give_w = pick(first, jnp.stack([pol_gate, pol_up]), jnp.stack([ref_gate, ref_up]))
    keep_d, give_d = pick(first, pol_down, ref_down)
    got_w = lax.ppermute(give_w, "core", SWAP)
    got_d = lax.ppermute(give_d, "core", SWAP)
    mlp_gain = jnp.where(first, pol_mlp_gain, ref_mlp_gain)
    partial = mlp_partial(group_rows, mlp_gain, keep_w[0], keep_w[1], keep_d) + mlp_partial(
        group_rows, mlp_gain, got_w[0], got_w[1], got_d
    )
    mixed = scatter_halving(partial)
    out = (pair_rows.astype(jnp.float32) + mixed).astype(jnp.bfloat16)
    final = gather_doubling(rms_rows(out, jnp.where(first, pol_final_gain, ref_final_gain)))
    mine_out = lax.dynamic_slice_in_dim(out, core * rows, rows, axis=0)
    sent_out = lax.ppermute(lax.dynamic_slice_in_dim(out, (1 - core) * rows, rows, axis=0), "core", SWAP)
    pol_out = jnp.where(first, mine_out, sent_out)
    ref_out = jnp.where(first, sent_out, mine_out)

    every = lax.all_gather(final, "grp", axis=0, tiled=True)
    keep_v, give_v = pick(first, pol_head, ref_head)
    got_v = lax.ppermute(give_v, "core", SWAP)
    voc_dev = pol_head.shape[0]
    positions = jnp.arange(every.shape[0], dtype=jnp.int32)
    base = group * per_group
    vocab = jnp.concatenate(
        [
            (base + member) * voc_dev + jnp.arange(voc_dev, dtype=jnp.int32),
            (base + partner) * voc_dev + jnp.arange(voc_dev, dtype=jnp.int32),
        ]
    )
    own_terms = jnp.stack(vocab_terms(every, jnp.concatenate([keep_v, got_v]), token_ids, vocab))
    other_terms = lax.ppermute(own_terms, "core", SWAP)
    state = jnp.where(first, jnp.stack([own_terms, other_terms]), jnp.stack([other_terms, own_terms]))
    size = lax.axis_size("zx")
    x_span = min(4, size)
    state = exchange_merge(state, "zx", x_span, 1)
    state = exchange_merge(state, "zx", size // x_span, x_span)
    state = exchange_merge(state, "grp", lax.axis_size("grp"), 1)
    logp = state[:, 2] - state[:, 0] - jnp.log(state[:, 1])
    rollout_ratio = rollout_totals(logp[0] - logp[1], positions, lengths)
    return (pol_out, ref_out, rollout_ratio)


def solution(mesh):
    groups, members = mesh.devices.shape
    split = Mesh(mesh.devices.reshape(groups, members // 2, 2), ("grp", "zx", "core"))
    rows = P(("grp", "zx", "core"), None)
    units = ("zx", "core")
    placed = (
        rows,
        rows,
        P(),
        P(),
        P(),
        P(),
        P(None, units),
        P(None, units),
        P(units, None),
        P(None, units),
        P(None, units),
        P(units, None),
        rows,
        rows,
        P(),
        P(),
    )
    return jax.shard_map(
        per_device,
        mesh=split,
        in_specs=placed,
        out_specs=(rows, rows, P()),
        check_vma=False,
    )
```

```python
import jax
import jax.numpy as jnp
from jax import lax
from jax.sharding import Mesh
from jax.sharding import PartitionSpec as P

SWAP = [(0, 1), (1, 0)]


def rms_rows(rows, gain):
    values = rows.astype(jnp.float32)
    scale = lax.rsqrt(jnp.mean(values * values, axis=-1, keepdims=True) + 1e-05)
    return (values * scale * gain.astype(jnp.float32)).astype(jnp.bfloat16)


def mlp_partial(piece, gain, w_gate, w_up, w_down):
    normed = rms_rows(piece, gain)
    gate = jnp.dot(normed, w_gate, preferred_element_type=jnp.float32)
    upper = jnp.dot(normed, w_up, preferred_element_type=jnp.float32)
    hidden = (jax.nn.silu(gate) * upper).astype(jnp.bfloat16)
    return jnp.dot(hidden, w_down, preferred_element_type=jnp.float32)


def vocab_terms(token_rows, head_rows, targets, vocab):
    logits = jnp.einsum("td,vd->tv", token_rows, head_rows, preferred_element_type=jnp.float32)
    peak = jnp.max(logits, axis=1)
    total = jnp.sum(jnp.exp(logits - peak[:, None]), axis=1)
    target = jnp.sum(jnp.where(targets[:, None] == vocab[None, :], logits, 0.0), axis=1)
    return (peak, total, target)


def merge_terms(lo, hi):
    peak = jnp.maximum(lo[:, 0], hi[:, 0])
    total = lo[:, 1] * jnp.exp(lo[:, 0] - peak) + hi[:, 1] * jnp.exp(hi[:, 0] - peak)
    return jnp.stack([peak, total, lo[:, 2] + hi[:, 2]], axis=1)


def rollout_totals(log_ratio, positions, lengths):
    ends = jnp.cumsum(lengths)
    owner = jnp.sum((positions[:, None] >= ends[None, :]).astype(jnp.int32), axis=1)
    onehot = (owner[:, None] == jnp.arange(lengths.shape[0], dtype=jnp.int32)[None, :]).astype(
        jnp.float32
    )
    return jnp.sum(log_ratio[:, None] * onehot, axis=0)


def zx_bits():
    size = lax.axis_size("zx")
    return [1 << k for k in reversed(range(size.bit_length() - 1))]


def exchange(held, bit):
    size = lax.axis_size("zx")
    return lax.ppermute(held, "zx", [(i, i ^ bit) for i in range(size)])


def double(held, bit, bits):
    dim = bits.index(bit)
    other = exchange(held, bit)
    low = (lax.axis_index("zx") & bit) == 0
    return jnp.concatenate([jnp.where(low, held, other), jnp.where(low, other, held)], axis=dim)


def halve(held, bit, bits):
    dim = bits.index(bit)
    lower = lax.slice_in_dim(held, 0, 1, axis=dim)
    upper = lax.slice_in_dim(held, 1, 2, axis=dim)
    low = (lax.axis_index("zx") & bit) == 0
    return jnp.where(low, lower, upper) + exchange(jnp.where(low, upper, lower), bit)


def split_columns(held):
    width = held.shape[-1] // 2
    return held[..., :width], held[..., width:]


def gather_doubling(block):
    bits = zx_bits()
    held = block.reshape((1,) * len(bits) + block.shape)
    far = [b for b in bits if b not in (1, 4)]
    for bit in far:
        held = double(held, bit, bits)
    if 1 in bits and 4 in bits:
        first, second = split_columns(held)
        first = double(first, 4, bits)
        second = double(second, 1, bits)
        first = double(first, 1, bits)
        second = double(second, 4, bits)
        held = jnp.concatenate([first, second], axis=-1)
    else:
        for bit in [b for b in bits if b in (1, 4)]:
            held = double(held, bit, bits)
    return held.reshape((-1,) + block.shape[1:])


def scatter_halving(full):
    bits = zx_bits()
    held = full.reshape((2,) * len(bits) + (-1,) + full.shape[1:])
    if 1 in bits and 4 in bits:
        first, second = split_columns(held)
        first = halve(first, 1, bits)
        second = halve(second, 4, bits)
        first = halve(first, 4, bits)
        second = halve(second, 1, bits)
        held = jnp.concatenate([first, second], axis=-1)
    else:
        for bit in [b for b in bits if b in (1, 4)]:
            held = halve(held, bit, bits)
    for bit in reversed([b for b in bits if b not in (1, 4)]):
        held = halve(held, bit, bits)
    return held.reshape((-1,) + full.shape[1:])


def pick(first, pol, ref):
    return jnp.where(first, pol, ref), jnp.where(first, ref, pol)


def per_device(
    pol_hidden,
    ref_hidden,
    pol_mlp_gain,
    ref_mlp_gain,
    pol_final_gain,
    ref_final_gain,
    pol_gate,
    pol_up,
    pol_down,
    ref_gate,
    ref_up,
    ref_down,
    pol_head,
    ref_head,
    token_ids,
    lengths,
):
    rows = pol_hidden.shape[0]
    core = lax.axis_index("core")
    spot = lax.axis_index("zx")
    group = lax.axis_index("grp")
    first = core == 0
    per_group = lax.axis_size("zx") * 2
    member = spot * 2 + core
    partner = spot * 2 + (1 - core)

    keep_w, give_w = pick(first, jnp.stack([pol_gate, pol_up]), jnp.stack([ref_gate, ref_up]))
    keep_d, give_d = pick(first, pol_down, ref_down)
    got_w = lax.ppermute(give_w, "core", SWAP)
    got_d = lax.ppermute(give_d, "core", SWAP)
    keep_h, give_h = pick(first, pol_hidden, ref_hidden)
    got_h = lax.ppermute(give_h, "core", SWAP)
    pair_rows = jnp.where(
        first, jnp.concatenate([keep_h, got_h]), jnp.concatenate([got_h, keep_h])
    )
    group_rows = gather_doubling(pair_rows)
    mlp_gain = jnp.where(first, pol_mlp_gain, ref_mlp_gain)
    partial = mlp_partial(group_rows, mlp_gain, keep_w[0], keep_w[1], keep_d) + mlp_partial(
        group_rows, mlp_gain, got_w[0], got_w[1], got_d
    )
    mixed = scatter_halving(partial)
    out = (pair_rows.astype(jnp.float32) + mixed).astype(jnp.bfloat16)
    final = gather_doubling(rms_rows(out, jnp.where(first, pol_final_gain, ref_final_gain)))
    mine_out = lax.dynamic_slice_in_dim(out, core * rows, rows, axis=0)
    sent_out = lax.ppermute(lax.dynamic_slice_in_dim(out, (1 - core) * rows, rows, axis=0), "core", SWAP)
    pol_out = jnp.where(first, mine_out, sent_out)
    ref_out = jnp.where(first, sent_out, mine_out)

    every = lax.all_gather(final, "grp", axis=0, tiled=True)
    keep_v, give_v = pick(first, pol_head, ref_head)
    got_v = lax.ppermute(give_v, "core", SWAP)
    voc_dev = pol_head.shape[0]
    positions = jnp.arange(every.shape[0], dtype=jnp.int32)
    base = group * per_group
    vocab = jnp.concatenate(
        [
            (base + member) * voc_dev + jnp.arange(voc_dev, dtype=jnp.int32),
            (base + partner) * voc_dev + jnp.arange(voc_dev, dtype=jnp.int32),
        ]
    )
    own_terms = jnp.stack(vocab_terms(every, jnp.concatenate([keep_v, got_v]), token_ids, vocab))
    other_terms = lax.ppermute(own_terms, "core", SWAP)
    state = jnp.where(first, jnp.stack([own_terms, other_terms]), jnp.stack([other_terms, own_terms]))
    rounds = [("zx", 1), ("zx", 2), ("zx", 4), ("zx", 8), ("zx", 16), ("grp", 1), ("grp", 2)]
    for axis, bit in rounds:
        size = lax.axis_size(axis)
        other = lax.ppermute(state, axis, [(i, i ^ bit) for i in range(size)])
        low = (lax.axis_index(axis) & bit) == 0
        state = merge_terms(jnp.where(low, state, other), jnp.where(low, other, state))
    logp = state[:, 2] - state[:, 0] - jnp.log(state[:, 1])
    rollout_ratio = rollout_totals(logp[0] - logp[1], positions, lengths)
    return (pol_out, ref_out, rollout_ratio)


def solution(mesh):
    groups, members = mesh.devices.shape
    split = Mesh(mesh.devices.reshape(groups, members // 2, 2), ("grp", "zx", "core"))
    rows = P(("grp", "zx", "core"), None)
    units = ("zx", "core")
    placed = (
        rows,
        rows,
        P(),
        P(),
        P(),
        P(),
        P(None, units),
        P(None, units),
        P(units, None),
        P(None, units),
        P(None, units),
        P(units, None),
        rows,
        rows,
        P(),
        P(),
    )
    return jax.shard_map(
        per_device,
        mesh=split,
        in_specs=placed,
        out_specs=(rows, rows, P()),
        check_vma=False,
    )
```

```python
import jax
import jax.numpy as jnp
from jax import lax
from jax.sharding import Mesh
from jax.sharding import PartitionSpec as P

SWAP = [(0, 1), (1, 0)]


def rms_rows(rows, gain):
    values = rows.astype(jnp.float32)
    scale = lax.rsqrt(jnp.mean(values * values, axis=-1, keepdims=True) + 1e-05)
    return (values * scale * gain.astype(jnp.float32)).astype(jnp.bfloat16)


def mlp_partial(piece, gain, w_gate, w_up, w_down):
    normed = rms_rows(piece, gain)
    gate = jnp.dot(normed, w_gate, preferred_element_type=jnp.float32)
    upper = jnp.dot(normed, w_up, preferred_element_type=jnp.float32)
    hidden = (jax.nn.silu(gate) * upper).astype(jnp.bfloat16)
    return jnp.dot(hidden, w_down, preferred_element_type=jnp.float32)


def vocab_terms(token_rows, head_rows, targets, vocab):
    logits = jnp.einsum("td,vd->tv", token_rows, head_rows, preferred_element_type=jnp.float32)
    peak = jnp.max(logits, axis=1)
    total = jnp.sum(jnp.exp(logits - peak[:, None]), axis=1)
    target = jnp.sum(jnp.where(targets[:, None] == vocab[None, :], logits, 0.0), axis=1)
    return (peak, total, target)


def merge_terms(lo, hi):
    peak = jnp.maximum(lo[:, 0], hi[:, 0])
    total = lo[:, 1] * jnp.exp(lo[:, 0] - peak) + hi[:, 1] * jnp.exp(hi[:, 0] - peak)
    return jnp.stack([peak, total, lo[:, 2] + hi[:, 2]], axis=1)


def rollout_totals(log_ratio, positions, lengths):
    ends = jnp.cumsum(lengths)
    owner = jnp.sum((positions[:, None] >= ends[None, :]).astype(jnp.int32), axis=1)
    onehot = (owner[:, None] == jnp.arange(lengths.shape[0], dtype=jnp.int32)[None, :]).astype(
        jnp.float32
    )
    return jnp.sum(log_ratio[:, None] * onehot, axis=0)


def zx_bits():
    size = lax.axis_size("zx")
    return [1 << k for k in reversed(range(size.bit_length() - 1))]


def partner_mask(bit):
    return 3 if bit == 2 else bit


def gather_doubling(block, orders=((16, 8, 1, 4, 2), (16, 1, 8, 2, 4))):
    bits = zx_bits()
    spot = lax.axis_index("zx")
    size = lax.axis_size("zx")
    width = block.shape[-1] // len(orders)
    parts = []
    for k in range(len(orders)):
        piece = lax.slice_in_dim(block, k * width, (k + 1) * width, axis=block.ndim - 1)
        parts.append(piece.reshape((1,) * len(bits) + piece.shape))
    for step in range(len(orders[0])):
        for k, order in enumerate(orders):
            bit = order[step]
            if bit not in bits:
                continue
            dim = bits.index(bit)
            held = parts[k]
            other = lax.ppermute(held, "zx", [(i, i ^ partner_mask(bit)) for i in range(size)])
            low = (spot & bit) == 0
            parts[k] = jnp.concatenate(
                [jnp.where(low, held, other), jnp.where(low, other, held)], axis=dim
            )
    rows = [p.reshape((-1,) + p.shape[len(bits) + 1 :]) for p in parts]
    return jnp.concatenate(rows, axis=-1)


def scatter_halving(full, orders=((2, 4, 1, 8, 16), (4, 2, 8, 1, 16))):
    bits = zx_bits()
    spot = lax.axis_index("zx")
    size = lax.axis_size("zx")
    width = full.shape[-1] // len(orders)
    parts = []
    for k in range(len(orders)):
        piece = lax.slice_in_dim(full, k * width, (k + 1) * width, axis=full.ndim - 1)
        parts.append(piece.reshape((2,) * len(bits) + (-1,) + piece.shape[1:]))
    for step in range(len(orders[0])):
        for k, order in enumerate(orders):
            bit = order[step]
            if bit not in bits:
                continue
            dim = bits.index(bit)
            held = parts[k]
            lower = lax.slice_in_dim(held, 0, 1, axis=dim)
            upper = lax.slice_in_dim(held, 1, 2, axis=dim)
            low = (spot & bit) == 0
            other = lax.ppermute(
                jnp.where(low, upper, lower), "zx", [(i, i ^ partner_mask(bit)) for i in range(size)]
            )
            parts[k] = jnp.where(low, lower, upper) + other
    rows = [p.reshape((-1,) + full.shape[1:-1] + (width,)) for p in parts]
    return jnp.concatenate(rows, axis=-1)


def pick(first, pol, ref):
    return jnp.where(first, pol, ref), jnp.where(first, ref, pol)


def per_device(
    pol_hidden,
    ref_hidden,
    pol_mlp_gain,
    ref_mlp_gain,
    pol_final_gain,
    ref_final_gain,
    pol_gate,
    pol_up,
    pol_down,
    ref_gate,
    ref_up,
    ref_down,
    pol_head,
    ref_head,
    token_ids,
    lengths,
):
    rows = pol_hidden.shape[0]
    core = lax.axis_index("core")
    spot = lax.axis_index("zx")
    group = lax.axis_index("grp")
    first = core == 0
    per_group = lax.axis_size("zx") * 2
    member = spot * 2 + core
    partner = spot * 2 + (1 - core)

    pol_w = (pol_gate, pol_up, pol_down)
    ref_w = (ref_gate, ref_up, ref_down)
    got_w = lax.ppermute(lax.cond(first, lambda: ref_w, lambda: pol_w), "core", SWAP)
    keep_h, give_h = pick(first, pol_hidden, ref_hidden)
    got_h = lax.ppermute(give_h, "core", SWAP)
    pair_rows = jnp.where(
        first, jnp.concatenate([keep_h, got_h]), jnp.concatenate([got_h, keep_h])
    )
    group_rows = gather_doubling(pair_rows)
    mlp_gain = jnp.where(first, pol_mlp_gain, ref_mlp_gain)
    partial = lax.cond(
        first,
        lambda: mlp_partial(group_rows, mlp_gain, *pol_w) + mlp_partial(group_rows, mlp_gain, *got_w),
        lambda: mlp_partial(group_rows, mlp_gain, *ref_w) + mlp_partial(group_rows, mlp_gain, *got_w),
    )
    mixed = scatter_halving(partial)
    out = (pair_rows.astype(jnp.float32) + mixed).astype(jnp.bfloat16)
    final = gather_doubling(rms_rows(out, jnp.where(first, pol_final_gain, ref_final_gain)))
    mine_out = lax.dynamic_slice_in_dim(out, core * rows, rows, axis=0)
    sent_out = lax.ppermute(lax.dynamic_slice_in_dim(out, (1 - core) * rows, rows, axis=0), "core", SWAP)
    pol_out = jnp.where(first, mine_out, sent_out)
    ref_out = jnp.where(first, sent_out, mine_out)

    every = lax.all_gather(final, "grp", axis=0, tiled=True)
    keep_v, give_v = pick(first, pol_head, ref_head)
    got_v = lax.ppermute(give_v, "core", SWAP)
    voc_dev = pol_head.shape[0]
    positions = jnp.arange(every.shape[0], dtype=jnp.int32)
    base = group * per_group
    vocab = jnp.concatenate(
        [
            (base + member) * voc_dev + jnp.arange(voc_dev, dtype=jnp.int32),
            (base + partner) * voc_dev + jnp.arange(voc_dev, dtype=jnp.int32),
        ]
    )
    own_terms = jnp.stack(vocab_terms(every, jnp.concatenate([keep_v, got_v]), token_ids, vocab))
    other_terms = lax.ppermute(own_terms, "core", SWAP)
    state = jnp.where(first, jnp.stack([own_terms, other_terms]), jnp.stack([other_terms, own_terms]))
    rounds = [("zx", 1), ("zx", 2), ("zx", 4), ("zx", 8), ("zx", 16), ("grp", 1), ("grp", 2)]
    for axis, bit in rounds:
        size = lax.axis_size(axis)
        other = lax.ppermute(state, axis, [(i, i ^ partner_mask(bit)) for i in range(size)])
        low = (lax.axis_index(axis) & bit) == 0
        state = merge_terms(jnp.where(low, state, other), jnp.where(low, other, state))
    logp = state[:, 2] - state[:, 0] - jnp.log(state[:, 1])
    rollout_ratio = rollout_totals(logp[0] - logp[1], positions, lengths)
    return (pol_out, ref_out, rollout_ratio)


def solution(mesh):
    groups, members = mesh.devices.shape
    split = Mesh(mesh.devices.reshape(groups, members // 2, 2), ("grp", "zx", "core"))
    rows = P(("grp", "zx", "core"), None)
    units = ("zx", "core")
    placed = (
        rows,
        rows,
        P(),
        P(),
        P(),
        P(),
        P(None, units),
        P(None, units),
        P(units, None),
        P(None, units),
        P(None, units),
        P(units, None),
        rows,
        rows,
        P(),
        P(),
    )
    return jax.shard_map(
        per_device,
        mesh=split,
        in_specs=placed,
        out_specs=(rows, rows, P()),
        check_vma=False,
    )
```

```python
import jax
import jax.numpy as jnp
from jax import lax
from jax.sharding import Mesh
from jax.sharding import PartitionSpec as P

SWAP = [(0, 1), (1, 0)]


def rms_rows(rows, gain):
    values = rows.astype(jnp.float32)
    scale = lax.rsqrt(jnp.mean(values * values, axis=-1, keepdims=True) + 1e-05)
    return (values * scale * gain.astype(jnp.float32)).astype(jnp.bfloat16)


def mlp_partial(piece, gain, w_gate, w_up, w_down):
    normed = rms_rows(piece, gain)
    gate = jnp.dot(normed, w_gate, preferred_element_type=jnp.float32)
    upper = jnp.dot(normed, w_up, preferred_element_type=jnp.float32)
    hidden = (jax.nn.silu(gate) * upper).astype(jnp.bfloat16)
    return jnp.dot(hidden, w_down, preferred_element_type=jnp.float32)


def vocab_terms(token_rows, head_rows, targets, vocab):
    logits = jnp.einsum("td,vd->tv", token_rows, head_rows, preferred_element_type=jnp.float32)
    peak = jnp.max(logits, axis=1)
    total = jnp.sum(jnp.exp(logits - peak[:, None]), axis=1)
    target = jnp.sum(jnp.where(targets[:, None] == vocab[None, :], logits, 0.0), axis=1)
    return (peak, total, target)


def merge_terms(lo, hi):
    peak = jnp.maximum(lo[:, 0], hi[:, 0])
    total = lo[:, 1] * jnp.exp(lo[:, 0] - peak) + hi[:, 1] * jnp.exp(hi[:, 0] - peak)
    return jnp.stack([peak, total, lo[:, 2] + hi[:, 2]], axis=1)


def rollout_totals(log_ratio, positions, lengths):
    ends = jnp.cumsum(lengths)
    owner = jnp.sum((positions[:, None] >= ends[None, :]).astype(jnp.int32), axis=1)
    onehot = (owner[:, None] == jnp.arange(lengths.shape[0], dtype=jnp.int32)[None, :]).astype(
        jnp.float32
    )
    return jnp.sum(log_ratio[:, None] * onehot, axis=0)


def zx_bits():
    size = lax.axis_size("zx")
    return [1 << k for k in reversed(range(size.bit_length() - 1))]


def partner_mask(bit):
    return 3 if bit == 2 else bit


def gather_doubling(block, orders=((16, 8, 1, 4, 2), (16, 1, 8, 2, 4))):
    bits = zx_bits()
    spot = lax.axis_index("zx")
    size = lax.axis_size("zx")
    width = block.shape[-1] // len(orders)
    parts = []
    for k in range(len(orders)):
        piece = lax.slice_in_dim(block, k * width, (k + 1) * width, axis=block.ndim - 1)
        parts.append(piece.reshape((1,) * len(bits) + piece.shape))
    for step in range(len(orders[0])):
        for k, order in enumerate(orders):
            bit = order[step]
            if bit not in bits:
                continue
            dim = bits.index(bit)
            held = parts[k]
            other = lax.ppermute(held, "zx", [(i, i ^ partner_mask(bit)) for i in range(size)])
            low = (spot & bit) == 0
            parts[k] = jnp.concatenate(
                [jnp.where(low, held, other), jnp.where(low, other, held)], axis=dim
            )
    rows = [p.reshape((-1,) + p.shape[len(bits) + 1 :]) for p in parts]
    return jnp.concatenate(rows, axis=-1)


def scatter_halving(full, orders=((2, 4, 1, 8, 16), (4, 2, 8, 1, 16))):
    bits = zx_bits()
    spot = lax.axis_index("zx")
    size = lax.axis_size("zx")
    width = full.shape[-1] // len(orders)
    parts = []
    for k in range(len(orders)):
        piece = lax.slice_in_dim(full, k * width, (k + 1) * width, axis=full.ndim - 1)
        parts.append(piece.reshape((2,) * len(bits) + (-1,) + piece.shape[1:]))
    for step in range(len(orders[0])):
        for k, order in enumerate(orders):
            bit = order[step]
            if bit not in bits:
                continue
            dim = bits.index(bit)
            held = parts[k]
            lower = lax.slice_in_dim(held, 0, 1, axis=dim)
            upper = lax.slice_in_dim(held, 1, 2, axis=dim)
            low = (spot & bit) == 0
            other = lax.ppermute(
                jnp.where(low, upper, lower), "zx", [(i, i ^ partner_mask(bit)) for i in range(size)]
            )
            parts[k] = jnp.where(low, lower, upper) + other
    rows = [p.reshape((-1,) + full.shape[1:-1] + (width,)) for p in parts]
    return jnp.concatenate(rows, axis=-1)


def pick(first, pol, ref):
    return jnp.where(first, pol, ref), jnp.where(first, ref, pol)


def per_device(
    pol_hidden,
    ref_hidden,
    pol_mlp_gain,
    ref_mlp_gain,
    pol_final_gain,
    ref_final_gain,
    pol_gate,
    pol_up,
    pol_down,
    ref_gate,
    ref_up,
    ref_down,
    pol_head,
    ref_head,
    token_ids,
    lengths,
):
    rows = pol_hidden.shape[0]
    core = lax.axis_index("core")
    spot = lax.axis_index("zx")
    group = lax.axis_index("grp")
    first = core == 0
    per_group = lax.axis_size("zx") * 2
    member = spot * 2 + core
    partner = spot * 2 + (1 - core)

    pol_w = (pol_gate, pol_up, pol_down)
    ref_w = (ref_gate, ref_up, ref_down)
    got_w = lax.ppermute(lax.cond(first, lambda: ref_w, lambda: pol_w), "core", SWAP)
    keep_h, give_h = pick(first, pol_hidden, ref_hidden)
    got_h = lax.ppermute(give_h, "core", SWAP)
    pair_rows = jnp.where(
        first, jnp.concatenate([keep_h, got_h]), jnp.concatenate([got_h, keep_h])
    )
    group_rows = gather_doubling(pair_rows)
    mlp_gain = jnp.where(first, pol_mlp_gain, ref_mlp_gain)
    units = pol_gate.shape[1]
    gate_up = jnp.concatenate(
        [jnp.where(first, pol_gate, ref_gate), got_w[0], jnp.where(first, pol_up, ref_up), got_w[1]],
        axis=1,
    )
    down = jnp.concatenate([jnp.where(first, pol_down, ref_down), got_w[2]], axis=0)
    normed = rms_rows(group_rows, mlp_gain)
    both = jnp.dot(normed, gate_up, preferred_element_type=jnp.float32)
    gate, upper = both[:, : 2 * units], both[:, 2 * units :]
    hidden = (jax.nn.silu(gate) * upper).astype(jnp.bfloat16)
    partial = jnp.dot(hidden, down, preferred_element_type=jnp.float32)
    mixed = scatter_halving(partial)
    out = (pair_rows.astype(jnp.float32) + mixed).astype(jnp.bfloat16)
    final = gather_doubling(rms_rows(out, jnp.where(first, pol_final_gain, ref_final_gain)))
    mine_out = lax.dynamic_slice_in_dim(out, core * rows, rows, axis=0)
    sent_out = lax.ppermute(lax.dynamic_slice_in_dim(out, (1 - core) * rows, rows, axis=0), "core", SWAP)
    pol_out = jnp.where(first, mine_out, sent_out)
    ref_out = jnp.where(first, sent_out, mine_out)

    every = lax.all_gather(final, "grp", axis=0, tiled=True)
    keep_v, give_v = pick(first, pol_head, ref_head)
    got_v = lax.ppermute(give_v, "core", SWAP)
    voc_dev = pol_head.shape[0]
    positions = jnp.arange(every.shape[0], dtype=jnp.int32)
    base = group * per_group
    vocab = jnp.concatenate(
        [
            (base + member) * voc_dev + jnp.arange(voc_dev, dtype=jnp.int32),
            (base + partner) * voc_dev + jnp.arange(voc_dev, dtype=jnp.int32),
        ]
    )
    own_terms = jnp.stack(vocab_terms(every, jnp.concatenate([keep_v, got_v]), token_ids, vocab))
    other_terms = lax.ppermute(own_terms, "core", SWAP)
    state = jnp.where(first, jnp.stack([own_terms, other_terms]), jnp.stack([other_terms, own_terms]))
    rounds = [("zx", 1), ("zx", 2), ("zx", 4), ("zx", 8), ("zx", 16), ("grp", 1), ("grp", 2)]
    for axis, bit in rounds:
        size = lax.axis_size(axis)
        other = lax.ppermute(state, axis, [(i, i ^ partner_mask(bit)) for i in range(size)])
        low = (lax.axis_index(axis) & bit) == 0
        state = merge_terms(jnp.where(low, state, other), jnp.where(low, other, state))
    logp = state[:, 2] - state[:, 0] - jnp.log(state[:, 1])
    rollout_ratio = rollout_totals(logp[0] - logp[1], positions, lengths)
    return (pol_out, ref_out, rollout_ratio)


def solution(mesh):
    groups, members = mesh.devices.shape
    split = Mesh(mesh.devices.reshape(groups, members // 2, 2), ("grp", "zx", "core"))
    rows = P(("grp", "zx", "core"), None)
    units = ("zx", "core")
    placed = (
        rows,
        rows,
        P(),
        P(),
        P(),
        P(),
        P(None, units),
        P(None, units),
        P(units, None),
        P(None, units),
        P(None, units),
        P(units, None),
        rows,
        rows,
        P(),
        P(),
    )
    return jax.shard_map(
        per_device,
        mesh=split,
        in_specs=placed,
        out_specs=(rows, rows, P()),
        check_vma=False,
    )
```

```python
import jax
import jax.numpy as jnp
from jax import lax
from jax.sharding import Mesh
from jax.sharding import PartitionSpec as P

SWAP = [(0, 1), (1, 0)]


def rms_rows(rows, gain):
    values = rows.astype(jnp.float32)
    scale = lax.rsqrt(jnp.mean(values * values, axis=-1, keepdims=True) + 1e-05)
    return (values * scale * gain.astype(jnp.float32)).astype(jnp.bfloat16)


def mlp_partial(piece, gain, w_gate, w_up, w_down):
    normed = rms_rows(piece, gain)
    gate = jnp.dot(normed, w_gate, preferred_element_type=jnp.float32)
    upper = jnp.dot(normed, w_up, preferred_element_type=jnp.float32)
    hidden = (jax.nn.silu(gate) * upper).astype(jnp.bfloat16)
    return jnp.dot(hidden, w_down, preferred_element_type=jnp.float32)


def vocab_terms(token_rows, head_rows, targets, vocab):
    logits = jnp.einsum("td,vd->tv", token_rows, head_rows, preferred_element_type=jnp.float32)
    peak = jnp.max(logits, axis=1)
    total = jnp.sum(jnp.exp(logits - peak[:, None]), axis=1)
    target = jnp.sum(jnp.where(targets[:, None] == vocab[None, :], logits, 0.0), axis=1)
    return (peak, total, target)


def merge_terms(lo, hi):
    peak = jnp.maximum(lo[:, 0], hi[:, 0])
    total = lo[:, 1] * jnp.exp(lo[:, 0] - peak) + hi[:, 1] * jnp.exp(hi[:, 0] - peak)
    return jnp.stack([peak, total, lo[:, 2] + hi[:, 2]], axis=1)


def rollout_totals(log_ratio, positions, lengths):
    ends = jnp.cumsum(lengths)
    owner = jnp.sum((positions[:, None] >= ends[None, :]).astype(jnp.int32), axis=1)
    onehot = (owner[:, None] == jnp.arange(lengths.shape[0], dtype=jnp.int32)[None, :]).astype(
        jnp.float32
    )
    return jnp.sum(log_ratio[:, None] * onehot, axis=0)


def zx_bits():
    size = lax.axis_size("zx")
    return [1 << k for k in reversed(range(size.bit_length() - 1))]


def partner_mask(bit):
    return 3 if bit == 2 else bit


def gather_doubling(block, orders=((16, 8, 1, 4, 2), (16, 1, 8, 2, 4))):
    bits = zx_bits()
    spot = lax.axis_index("zx")
    size = lax.axis_size("zx")
    width = block.shape[-1] // len(orders)
    parts = []
    for k in range(len(orders)):
        piece = lax.slice_in_dim(block, k * width, (k + 1) * width, axis=block.ndim - 1)
        parts.append(piece.reshape((1,) * len(bits) + piece.shape))
    for step in range(len(orders[0])):
        for k, order in enumerate(orders):
            bit = order[step]
            if bit not in bits:
                continue
            dim = bits.index(bit)
            held = parts[k]
            other = lax.ppermute(held, "zx", [(i, i ^ partner_mask(bit)) for i in range(size)])
            low = (spot & bit) == 0
            parts[k] = jnp.concatenate(
                [jnp.where(low, held, other), jnp.where(low, other, held)], axis=dim
            )
    rows = [p.reshape((-1,) + p.shape[len(bits) + 1 :]) for p in parts]
    return jnp.concatenate(rows, axis=-1)


def scatter_halving(full, orders=((2, 4, 1, 8, 16), (4, 2, 8, 1, 16))):
    bits = zx_bits()
    spot = lax.axis_index("zx")
    size = lax.axis_size("zx")
    width = full.shape[-1] // len(orders)
    parts = []
    for k in range(len(orders)):
        piece = lax.slice_in_dim(full, k * width, (k + 1) * width, axis=full.ndim - 1)
        parts.append(piece.reshape((2,) * len(bits) + (-1,) + piece.shape[1:]))
    for step in range(len(orders[0])):
        for k, order in enumerate(orders):
            bit = order[step]
            if bit not in bits:
                continue
            dim = bits.index(bit)
            held = parts[k]
            lower = lax.slice_in_dim(held, 0, 1, axis=dim)
            upper = lax.slice_in_dim(held, 1, 2, axis=dim)
            low = (spot & bit) == 0
            other = lax.ppermute(
                jnp.where(low, upper, lower), "zx", [(i, i ^ partner_mask(bit)) for i in range(size)]
            )
            parts[k] = jnp.where(low, lower, upper) + other
    rows = [p.reshape((-1,) + full.shape[1:-1] + (width,)) for p in parts]
    return jnp.concatenate(rows, axis=-1)


def pick(first, pol, ref):
    return jnp.where(first, pol, ref), jnp.where(first, ref, pol)


def per_device(
    pol_hidden,
    ref_hidden,
    pol_mlp_gain,
    ref_mlp_gain,
    pol_final_gain,
    ref_final_gain,
    pol_gate,
    pol_up,
    pol_down,
    ref_gate,
    ref_up,
    ref_down,
    pol_head,
    ref_head,
    token_ids,
    lengths,
):
    rows = pol_hidden.shape[0]
    core = lax.axis_index("core")
    spot = lax.axis_index("zx")
    group = lax.axis_index("grp")
    first = core == 0
    per_group = lax.axis_size("zx") * 2
    member = spot * 2 + core
    partner = spot * 2 + (1 - core)

    pol_w = (pol_gate, pol_up, pol_down)
    ref_w = (ref_gate, ref_up, ref_down)
    got_pol = lax.ppermute(pol_w, "core", [(1, 0)])
    got_ref = lax.ppermute(ref_w, "core", [(0, 1)])
    got_w = [jnp.where(first, p, r) for p, r in zip(got_pol, got_ref)]
    keep_h, give_h = pick(first, pol_hidden, ref_hidden)
    got_h = lax.ppermute(give_h, "core", SWAP)
    pair_rows = jnp.where(
        first, jnp.concatenate([keep_h, got_h]), jnp.concatenate([got_h, keep_h])
    )
    group_rows = gather_doubling(pair_rows)
    mlp_gain = jnp.where(first, pol_mlp_gain, ref_mlp_gain)
    units = pol_gate.shape[1]
    gate_up = jnp.concatenate(
        [jnp.where(first, pol_gate, ref_gate), got_w[0], jnp.where(first, pol_up, ref_up), got_w[1]],
        axis=1,
    )
    down = jnp.concatenate([jnp.where(first, pol_down, ref_down), got_w[2]], axis=0)
    normed = rms_rows(group_rows, mlp_gain)
    both = jnp.dot(normed, gate_up, preferred_element_type=jnp.float32)
    gate, upper = both[:, : 2 * units], both[:, 2 * units :]
    hidden = (jax.nn.silu(gate) * upper).astype(jnp.bfloat16)
    partial = jnp.dot(hidden, down, preferred_element_type=jnp.float32)
    mixed = scatter_halving(partial)
    out = (pair_rows.astype(jnp.float32) + mixed).astype(jnp.bfloat16)
    final = gather_doubling(rms_rows(out, jnp.where(first, pol_final_gain, ref_final_gain)))
    mine_out = lax.dynamic_slice_in_dim(out, core * rows, rows, axis=0)
    sent_out = lax.ppermute(lax.dynamic_slice_in_dim(out, (1 - core) * rows, rows, axis=0), "core", SWAP)
    pol_out = jnp.where(first, mine_out, sent_out)
    ref_out = jnp.where(first, sent_out, mine_out)

    every = lax.all_gather(final, "grp", axis=0, tiled=True)
    keep_v = jnp.where(first, pol_head, ref_head)
    got_v = jnp.where(
        first,
        lax.ppermute(pol_head, "core", [(1, 0)]),
        lax.ppermute(ref_head, "core", [(0, 1)]),
    )
    voc_dev = pol_head.shape[0]
    positions = jnp.arange(every.shape[0], dtype=jnp.int32)
    base = group * per_group
    vocab = jnp.concatenate(
        [
            (base + member) * voc_dev + jnp.arange(voc_dev, dtype=jnp.int32),
            (base + partner) * voc_dev + jnp.arange(voc_dev, dtype=jnp.int32),
        ]
    )
    own_terms = jnp.stack(vocab_terms(every, jnp.concatenate([keep_v, got_v]), token_ids, vocab))
    other_terms = lax.ppermute(own_terms, "core", SWAP)
    state = jnp.where(first, jnp.stack([own_terms, other_terms]), jnp.stack([other_terms, own_terms]))
    rounds = [("zx", 1), ("zx", 2), ("zx", 4), ("zx", 8), ("zx", 16), ("grp", 1), ("grp", 2)]
    for axis, bit in rounds:
        size = lax.axis_size(axis)
        other = lax.ppermute(state, axis, [(i, i ^ partner_mask(bit)) for i in range(size)])
        low = (lax.axis_index(axis) & bit) == 0
        state = merge_terms(jnp.where(low, state, other), jnp.where(low, other, state))
    logp = state[:, 2] - state[:, 0] - jnp.log(state[:, 1])
    rollout_ratio = rollout_totals(logp[0] - logp[1], positions, lengths)
    return (pol_out, ref_out, rollout_ratio)


def solution(mesh):
    groups, members = mesh.devices.shape
    split = Mesh(mesh.devices.reshape(groups, members // 2, 2), ("grp", "zx", "core"))
    rows = P(("grp", "zx", "core"), None)
    units = ("zx", "core")
    placed = (
        rows,
        rows,
        P(),
        P(),
        P(),
        P(),
        P(None, units),
        P(None, units),
        P(units, None),
        P(None, units),
        P(None, units),
        P(units, None),
        rows,
        rows,
        P(),
        P(),
    )
    return jax.shard_map(
        per_device,
        mesh=split,
        in_specs=placed,
        out_specs=(rows, rows, P()),
        check_vma=False,
    )
```

```python
import jax
import jax.numpy as jnp
from jax import lax
from jax.sharding import Mesh
from jax.sharding import PartitionSpec as P

SWAP = [(0, 1), (1, 0)]


def rms_rows(rows, gain):
    values = rows.astype(jnp.float32)
    scale = lax.rsqrt(jnp.mean(values * values, axis=-1, keepdims=True) + 1e-05)
    return (values * scale * gain.astype(jnp.float32)).astype(jnp.bfloat16)


def mlp_partial(piece, gain, w_gate, w_up, w_down):
    normed = rms_rows(piece, gain)
    gate = jnp.dot(normed, w_gate, preferred_element_type=jnp.float32)
    upper = jnp.dot(normed, w_up, preferred_element_type=jnp.float32)
    hidden = (jax.nn.silu(gate) * upper).astype(jnp.bfloat16)
    return jnp.dot(hidden, w_down, preferred_element_type=jnp.float32)


def vocab_terms(token_rows, head_rows, targets, vocab):
    logits = jnp.einsum("td,vd->tv", token_rows, head_rows, preferred_element_type=jnp.float32)
    peak = jnp.max(logits, axis=1)
    total = jnp.sum(jnp.exp(logits - peak[:, None]), axis=1)
    target = jnp.sum(jnp.where(targets[:, None] == vocab[None, :], logits, 0.0), axis=1)
    return (peak, total, target)


def merge_terms(lo, hi):
    peak = jnp.maximum(lo[:, 0], hi[:, 0])
    total = lo[:, 1] * jnp.exp(lo[:, 0] - peak) + hi[:, 1] * jnp.exp(hi[:, 0] - peak)
    return jnp.stack([peak, total, lo[:, 2] + hi[:, 2]], axis=1)


def rollout_totals(log_ratio, positions, lengths):
    ends = jnp.cumsum(lengths)
    owner = jnp.sum((positions[:, None] >= ends[None, :]).astype(jnp.int32), axis=1)
    onehot = (owner[:, None] == jnp.arange(lengths.shape[0], dtype=jnp.int32)[None, :]).astype(
        jnp.float32
    )
    return jnp.sum(log_ratio[:, None] * onehot, axis=0)


def zx_bits():
    size = lax.axis_size("zx")
    return [1 << k for k in reversed(range(size.bit_length() - 1))]


def partner_mask(bit):
    return 3 if bit == 2 else bit


def gather_doubling(block, orders=((16, 8, 1, 4, 2), (16, 1, 8, 2, 4))):
    bits = zx_bits()
    spot = lax.axis_index("zx")
    size = lax.axis_size("zx")
    width = block.shape[-1] // len(orders)
    parts = []
    for k in range(len(orders)):
        piece = lax.slice_in_dim(block, k * width, (k + 1) * width, axis=block.ndim - 1)
        parts.append(piece.reshape((1,) * len(bits) + piece.shape))
    for step in range(len(orders[0])):
        for k, order in enumerate(orders):
            bit = order[step]
            if bit not in bits:
                continue
            dim = bits.index(bit)
            held = parts[k]
            other = lax.ppermute(held, "zx", [(i, i ^ partner_mask(bit)) for i in range(size)])
            low = (spot & bit) == 0
            parts[k] = jnp.concatenate(
                [jnp.where(low, held, other), jnp.where(low, other, held)], axis=dim
            )
    rows = [p.reshape((-1,) + p.shape[len(bits) + 1 :]) for p in parts]
    return jnp.concatenate(rows, axis=-1)


def scatter_halving(full, orders=((2, 4, 1, 8, 16), (4, 2, 8, 1, 16))):
    bits = zx_bits()
    spot = lax.axis_index("zx")
    size = lax.axis_size("zx")
    width = full.shape[-1] // len(orders)
    parts = []
    for k in range(len(orders)):
        piece = lax.slice_in_dim(full, k * width, (k + 1) * width, axis=full.ndim - 1)
        parts.append(piece.reshape((2,) * len(bits) + (-1,) + piece.shape[1:]))
    for step in range(len(orders[0])):
        for k, order in enumerate(orders):
            bit = order[step]
            if bit not in bits:
                continue
            dim = bits.index(bit)
            held = parts[k]
            lower = lax.slice_in_dim(held, 0, 1, axis=dim)
            upper = lax.slice_in_dim(held, 1, 2, axis=dim)
            low = (spot & bit) == 0
            other = lax.ppermute(
                jnp.where(low, upper, lower), "zx", [(i, i ^ partner_mask(bit)) for i in range(size)]
            )
            parts[k] = jnp.where(low, lower, upper) + other
    rows = [p.reshape((-1,) + full.shape[1:-1] + (width,)) for p in parts]
    return jnp.concatenate(rows, axis=-1)


def pick(first, pol, ref):
    return jnp.where(first, pol, ref), jnp.where(first, ref, pol)


def per_device(
    pol_hidden,
    ref_hidden,
    pol_mlp_gain,
    ref_mlp_gain,
    pol_final_gain,
    ref_final_gain,
    pol_gate,
    pol_up,
    pol_down,
    ref_gate,
    ref_up,
    ref_down,
    pol_head,
    ref_head,
    token_ids,
    lengths,
):
    rows = pol_hidden.shape[0]
    core = lax.axis_index("core")
    spot = lax.axis_index("zx")
    group = lax.axis_index("grp")
    first = core == 0
    per_group = lax.axis_size("zx") * 2
    member = spot * 2 + core
    partner = spot * 2 + (1 - core)

    pol_w = (pol_gate, pol_up, pol_down)
    ref_w = (ref_gate, ref_up, ref_down)
    got_w = lax.ppermute(lax.cond(first, lambda: ref_w, lambda: pol_w), "core", SWAP)
    keep_h, give_h = pick(first, pol_hidden, ref_hidden)
    got_h = lax.ppermute(give_h, "core", SWAP)
    pair_rows = jnp.where(
        first, jnp.concatenate([keep_h, got_h]), jnp.concatenate([got_h, keep_h])
    )
    group_rows = gather_doubling(pair_rows)
    mlp_gain = jnp.where(first, pol_mlp_gain, ref_mlp_gain)
    units = pol_gate.shape[1]
    gate_up = jnp.concatenate(
        [jnp.where(first, pol_gate, ref_gate), got_w[0], jnp.where(first, pol_up, ref_up), got_w[1]],
        axis=1,
    )
    down = jnp.concatenate([jnp.where(first, pol_down, ref_down), got_w[2]], axis=0)
    normed = rms_rows(group_rows, mlp_gain)
    both = jnp.dot(normed, gate_up, preferred_element_type=jnp.float32)
    gate, upper = both[:, : 2 * units], both[:, 2 * units :]
    hidden = (jax.nn.silu(gate) * upper).astype(jnp.bfloat16)
    partial = jnp.dot(hidden, down, preferred_element_type=jnp.float32)
    mixed = scatter_halving(partial)
    mixed, pol_head, ref_head = lax.optimization_barrier((mixed, pol_head, ref_head))
    out = (pair_rows.astype(jnp.float32) + mixed).astype(jnp.bfloat16)
    final = gather_doubling(rms_rows(out, jnp.where(first, pol_final_gain, ref_final_gain)))
    mine_out = lax.dynamic_slice_in_dim(out, core * rows, rows, axis=0)
    sent_out = lax.ppermute(lax.dynamic_slice_in_dim(out, (1 - core) * rows, rows, axis=0), "core", SWAP)
    pol_out = jnp.where(first, mine_out, sent_out)
    ref_out = jnp.where(first, sent_out, mine_out)

    every = lax.all_gather(final, "grp", axis=0, tiled=True)
    keep_v, give_v = pick(first, pol_head, ref_head)
    got_v = lax.ppermute(give_v, "core", SWAP)
    voc_dev = pol_head.shape[0]
    positions = jnp.arange(every.shape[0], dtype=jnp.int32)
    base = group * per_group
    vocab = jnp.concatenate(
        [
            (base + member) * voc_dev + jnp.arange(voc_dev, dtype=jnp.int32),
            (base + partner) * voc_dev + jnp.arange(voc_dev, dtype=jnp.int32),
        ]
    )
    own_terms = jnp.stack(vocab_terms(every, jnp.concatenate([keep_v, got_v]), token_ids, vocab))
    other_terms = lax.ppermute(own_terms, "core", SWAP)
    state = jnp.where(first, jnp.stack([own_terms, other_terms]), jnp.stack([other_terms, own_terms]))
    rounds = [("zx", 1), ("zx", 2), ("zx", 4), ("zx", 8), ("zx", 16), ("grp", 1), ("grp", 2)]
    for axis, bit in rounds:
        size = lax.axis_size(axis)
        other = lax.ppermute(state, axis, [(i, i ^ partner_mask(bit)) for i in range(size)])
        low = (lax.axis_index(axis) & bit) == 0
        state = merge_terms(jnp.where(low, state, other), jnp.where(low, other, state))
    logp = state[:, 2] - state[:, 0] - jnp.log(state[:, 1])
    rollout_ratio = rollout_totals(logp[0] - logp[1], positions, lengths)
    return (pol_out, ref_out, rollout_ratio)


def solution(mesh):
    groups, members = mesh.devices.shape
    split = Mesh(mesh.devices.reshape(groups, members // 2, 2), ("grp", "zx", "core"))
    rows = P(("grp", "zx", "core"), None)
    units = ("zx", "core")
    placed = (
        rows,
        rows,
        P(),
        P(),
        P(),
        P(),
        P(None, units),
        P(None, units),
        P(units, None),
        P(None, units),
        P(None, units),
        P(units, None),
        rows,
        rows,
        P(),
        P(),
    )
    return jax.shard_map(
        per_device,
        mesh=split,
        in_specs=placed,
        out_specs=(rows, rows, P()),
        check_vma=False,
    )
```

```python
import jax
import jax.numpy as jnp
from jax import lax
from jax.sharding import Mesh
from jax.sharding import PartitionSpec as P

SWAP = [(0, 1), (1, 0)]


def rms_rows(rows, gain):
    values = rows.astype(jnp.float32)
    scale = lax.rsqrt(jnp.mean(values * values, axis=-1, keepdims=True) + 1e-05)
    return (values * scale * gain.astype(jnp.float32)).astype(jnp.bfloat16)


def mlp_partial(piece, gain, w_gate, w_up, w_down):
    normed = rms_rows(piece, gain)
    gate = jnp.dot(normed, w_gate, preferred_element_type=jnp.float32)
    upper = jnp.dot(normed, w_up, preferred_element_type=jnp.float32)
    hidden = (jax.nn.silu(gate) * upper).astype(jnp.bfloat16)
    return jnp.dot(hidden, w_down, preferred_element_type=jnp.float32)


def vocab_terms(token_parts, head_rows, targets, vocab):
    width = token_parts[0].shape[1]
    logits = sum(
        jnp.einsum(
            "td,vd->tv", part, head_rows[:, k * width : (k + 1) * width], preferred_element_type=jnp.float32
        )
        for k, part in enumerate(token_parts)
    )
    peak = jnp.max(logits, axis=1)
    total = jnp.sum(jnp.exp(logits - peak[:, None]), axis=1)
    target = jnp.sum(jnp.where(targets[:, None] == vocab[None, :], logits, 0.0), axis=1)
    return (peak, total, target)


def merge_terms(lo, hi):
    peak = jnp.maximum(lo[:, 0], hi[:, 0])
    total = lo[:, 1] * jnp.exp(lo[:, 0] - peak) + hi[:, 1] * jnp.exp(hi[:, 0] - peak)
    return jnp.stack([peak, total, lo[:, 2] + hi[:, 2]], axis=1)


def rollout_totals(log_ratio, positions, lengths):
    ends = jnp.cumsum(lengths)
    owner = jnp.sum((positions[:, None] >= ends[None, :]).astype(jnp.int32), axis=1)
    onehot = (owner[:, None] == jnp.arange(lengths.shape[0], dtype=jnp.int32)[None, :]).astype(
        jnp.float32
    )
    return jnp.sum(log_ratio[:, None] * onehot, axis=0)


def zx_bits():
    size = lax.axis_size("zx")
    return [1 << k for k in reversed(range(size.bit_length() - 1))]


def partner_mask(bit):
    return 3 if bit == 2 else bit


def gather_doubling(block, orders=((16, 8, 1, 4, 2), (16, 1, 8, 2, 4)), joined=True):
    bits = zx_bits()
    spot = lax.axis_index("zx")
    size = lax.axis_size("zx")
    width = block.shape[-1] // len(orders)
    parts = []
    for k in range(len(orders)):
        piece = lax.slice_in_dim(block, k * width, (k + 1) * width, axis=block.ndim - 1)
        parts.append(piece.reshape((1,) * len(bits) + piece.shape))
    for step in range(len(orders[0])):
        for k, order in enumerate(orders):
            bit = order[step]
            if bit not in bits:
                continue
            dim = bits.index(bit)
            held = parts[k]
            other = lax.ppermute(held, "zx", [(i, i ^ partner_mask(bit)) for i in range(size)])
            low = (spot & bit) == 0
            parts[k] = jnp.concatenate(
                [jnp.where(low, held, other), jnp.where(low, other, held)], axis=dim
            )
    rows = [p.reshape((-1,) + p.shape[len(bits) + 1 :]) for p in parts]
    return jnp.concatenate(rows, axis=-1) if joined else rows


def scatter_halving(full, orders=((2, 4, 1, 8, 16), (4, 2, 8, 1, 16))):
    bits = zx_bits()
    spot = lax.axis_index("zx")
    size = lax.axis_size("zx")
    width = full.shape[-1] // len(orders)
    parts = []
    for k in range(len(orders)):
        piece = lax.slice_in_dim(full, k * width, (k + 1) * width, axis=full.ndim - 1)
        parts.append(piece.reshape((2,) * len(bits) + (-1,) + piece.shape[1:]))
    for step in range(len(orders[0])):
        for k, order in enumerate(orders):
            bit = order[step]
            if bit not in bits:
                continue
            dim = bits.index(bit)
            held = parts[k]
            lower = lax.slice_in_dim(held, 0, 1, axis=dim)
            upper = lax.slice_in_dim(held, 1, 2, axis=dim)
            low = (spot & bit) == 0
            other = lax.ppermute(
                jnp.where(low, upper, lower), "zx", [(i, i ^ partner_mask(bit)) for i in range(size)]
            )
            parts[k] = jnp.where(low, lower, upper) + other
    rows = [p.reshape((-1,) + full.shape[1:-1] + (width,)) for p in parts]
    return jnp.concatenate(rows, axis=-1)


def pick(first, pol, ref):
    return jnp.where(first, pol, ref), jnp.where(first, ref, pol)


def per_device(
    pol_hidden,
    ref_hidden,
    pol_mlp_gain,
    ref_mlp_gain,
    pol_final_gain,
    ref_final_gain,
    pol_gate,
    pol_up,
    pol_down,
    ref_gate,
    ref_up,
    ref_down,
    pol_head,
    ref_head,
    token_ids,
    lengths,
):
    rows = pol_hidden.shape[0]
    core = lax.axis_index("core")
    spot = lax.axis_index("zx")
    group = lax.axis_index("grp")
    first = core == 0
    per_group = lax.axis_size("zx") * 2
    member = spot * 2 + core
    partner = spot * 2 + (1 - core)

    pol_w = (pol_gate, pol_up, pol_down)
    ref_w = (ref_gate, ref_up, ref_down)
    got_w = lax.ppermute(lax.cond(first, lambda: ref_w, lambda: pol_w), "core", SWAP)
    keep_h, give_h = pick(first, pol_hidden, ref_hidden)
    got_h = lax.ppermute(give_h, "core", SWAP)
    pair_rows = jnp.where(
        first, jnp.concatenate([keep_h, got_h]), jnp.concatenate([got_h, keep_h])
    )
    group_rows = gather_doubling(pair_rows)
    mlp_gain = jnp.where(first, pol_mlp_gain, ref_mlp_gain)
    units = pol_gate.shape[1]
    gate_up = jnp.concatenate(
        [jnp.where(first, pol_gate, ref_gate), got_w[0], jnp.where(first, pol_up, ref_up), got_w[1]],
        axis=1,
    )
    down = jnp.concatenate([jnp.where(first, pol_down, ref_down), got_w[2]], axis=0)
    normed = rms_rows(group_rows, mlp_gain)
    both = jnp.dot(normed, gate_up, preferred_element_type=jnp.float32)
    gate, upper = both[:, : 2 * units], both[:, 2 * units :]
    hidden = (jax.nn.silu(gate) * upper).astype(jnp.bfloat16)
    partial = jnp.dot(hidden, down, preferred_element_type=jnp.float32)
    mixed = scatter_halving(partial)
    out = (pair_rows.astype(jnp.float32) + mixed).astype(jnp.bfloat16)
    final = gather_doubling(rms_rows(out, jnp.where(first, pol_final_gain, ref_final_gain)), joined=False)
    mine_out = lax.dynamic_slice_in_dim(out, core * rows, rows, axis=0)
    sent_out = lax.ppermute(lax.dynamic_slice_in_dim(out, (1 - core) * rows, rows, axis=0), "core", SWAP)
    pol_out = jnp.where(first, mine_out, sent_out)
    ref_out = jnp.where(first, sent_out, mine_out)

    every = [lax.all_gather(part, "grp", axis=0, tiled=True) for part in final]
    keep_v, give_v = pick(first, pol_head, ref_head)
    got_v = lax.ppermute(give_v, "core", SWAP)
    voc_dev = pol_head.shape[0]
    positions = jnp.arange(every[0].shape[0], dtype=jnp.int32)
    base = group * per_group
    vocab = jnp.concatenate(
        [
            (base + member) * voc_dev + jnp.arange(voc_dev, dtype=jnp.int32),
            (base + partner) * voc_dev + jnp.arange(voc_dev, dtype=jnp.int32),
        ]
    )
    own_terms = jnp.stack(vocab_terms(every, jnp.concatenate([keep_v, got_v]), token_ids, vocab))
    other_terms = lax.ppermute(own_terms, "core", SWAP)
    state = jnp.where(first, jnp.stack([own_terms, other_terms]), jnp.stack([other_terms, own_terms]))
    rounds = [("zx", 1), ("zx", 2), ("zx", 4), ("zx", 8), ("zx", 16), ("grp", 1), ("grp", 2)]
    for axis, bit in rounds:
        size = lax.axis_size(axis)
        other = lax.ppermute(state, axis, [(i, i ^ partner_mask(bit)) for i in range(size)])
        low = (lax.axis_index(axis) & bit) == 0
        state = merge_terms(jnp.where(low, state, other), jnp.where(low, other, state))
    logp = state[:, 2] - state[:, 0] - jnp.log(state[:, 1])
    rollout_ratio = rollout_totals(logp[0] - logp[1], positions, lengths)
    return (pol_out, ref_out, rollout_ratio)


def solution(mesh):
    groups, members = mesh.devices.shape
    split = Mesh(mesh.devices.reshape(groups, members // 2, 2), ("grp", "zx", "core"))
    rows = P(("grp", "zx", "core"), None)
    units = ("zx", "core")
    placed = (
        rows,
        rows,
        P(),
        P(),
        P(),
        P(),
        P(None, units),
        P(None, units),
        P(units, None),
        P(None, units),
        P(None, units),
        P(units, None),
        rows,
        rows,
        P(),
        P(),
    )
    return jax.shard_map(
        per_device,
        mesh=split,
        in_specs=placed,
        out_specs=(rows, rows, P()),
        check_vma=False,
    )
```
